256 devices in a mesh: dp: 32 (over y, z), fsdp: 8 (over x, core).
Axes of the slice: x: 4, y: 4, z: 8, core: 2. Of those that a mesh axis runs over, the one named last changes fastest.
Arguments:
- prefill_tokens: bfloat16 [16384, 2048], P('dp'), may hold values from -3 to 3
- decode_tokens: bfloat16 [128, 2048], P('dp'), may hold values from -3 to 3
- query_weight: bfloat16 [2048, 2048], P('dp', 'fsdp'), may hold values from -0.125 to 0.125
- key_weight: bfloat16 [2048, 2048], P('dp', 'fsdp'), may hold values from -0.125 to 0.125
- value_weight: bfloat16 [2048, 2048], P('dp', 'fsdp'), may hold values from -0.125 to 0.125
- out_weight: bfloat16 [2048, 2048], P('fsdp', 'dp'), may hold values from -0.125 to 0.125
- prior_keys: bfloat16 [32, 2048, 2048], P('dp', None, 'fsdp'), may hold values from -480 to 480
- prior_values: bfloat16 [32, 2048, 2048], P('dp', None, 'fsdp'), may hold values from -6 to 6
- prior_length: int32 [32], P('dp'), may hold values from 0 to 2048, as said below
- pool_keys: bfloat16 [1536, 128, 2048], P('dp', None, 'fsdp'), may hold values from -480 to 480
- pool_values: bfloat16 [1536, 128, 2048], P('dp', None, 'fsdp'), may hold values from -6 to 6
- page_slots: int32 [1536], replicated, may hold values from 0 to 1535, each once
- page_counts: int32 [128], replicated, may hold values from 1 to 128, 1536 in all
- last_fill: int32 [128], replicated, may hold values from 1 to 128
- decode_request: int32 [128], replicated, may hold values from 0 to 127, each once
Outputs:
- mixed_prefill: bfloat16 [16384, 2048], P('dp', 'fsdp')
- mixed_decode: bfloat16 [128, 2048], P('dp', 'fsdp')
The draws below stay inside these ranges and needn't reach their ends.
Inputs may be any that keep to these rules, and one draw needn't show every extreme that they name: `prior_length`: one prefill request's prior fills all 2048 slots. Request r owns the logical pages first_page[r] to first_page[r] + page_counts[r] - 1; the counts sum to 1536, and some request has exactly 128 pages. A permutation: pool slot page_slots[k] holds logical page k. `decode_request`: A permutation of the decode requests.
All inputs are finite; a program needn't handle non-finite values.
Results may differ from the reference program's by a relative error of at most 0.015.
The reference program's roundings to bfloat16 on the way count: a program that leaves them out, or rounds other values in their place, can miss the bound.
Values may be sent and summed in bfloat16 or wider, within the bound.
No kernel may reach another device: no remote copies, remote signals or barrier semaphores. Data moves between devices by JAX's collectives and lax.ppermute only.
A program may use at most 128 MiB of HBM per device.

```python
import math
import jax
import jax.numpy as jnp
import numpy as np
from jax import lax

D = 2048
HEADS = 16
HEAD = 128
PAGE = 128
MAXP = 128
GROUP = 512
PRIOR_MAX = 2048
R_PRE = 32
PRE_TOKENS = 16384
R_DEC = 128
POOL = 1536


def heavy_rows(key, shape):
    base = 2.0 * jax.random.normal(jax.random.fold_in(key, 11), shape, jnp.float32)
    base = jnp.clip(base, -12.0, 12.0)
    return base


def draw_prior_keys(key, part):
    return heavy_rows(key, (R_PRE, PRIOR_MAX, D)).astype(jnp.bfloat16)


def draw_pool_keys(key, part):
    return heavy_rows(jax.random.fold_in(key, 5), (POOL, PAGE, D)).astype(jnp.bfloat16)


def draw_prior_length(key, part):
    values = jax.random.randint(jax.random.fold_in(key, 21), (R_PRE,), 0, PRIOR_MAX + 1)
    chosen = jax.random.randint(jax.random.fold_in(key, 22), (), 0, R_PRE)
    return jnp.where(jnp.arange(R_PRE) == chosen, PRIOR_MAX, values).astype(jnp.int32)


def set_ends(array, key, low, largest):
    extent = array.shape
    spot = [jax.random.randint(jax.random.fold_in(key, axis), (), 0, extent[axis]) for axis in range(len(extent))]
    array = array.at[tuple(spot)].set(low)
    longest = extent.index(max(extent))
    spot[longest] = (spot[longest] + 1) % extent[longest]
    return array.at[tuple(spot)].set(largest)


def block_scale(key, dims, shards, least, high):
    def one(axis_at, shards_of):
        heights = jax.random.uniform(jax.random.fold_in(jax.random.fold_in(key, 6), axis_at), (shards_of,), jnp.float32, least / len(shards), high / len(shards))
        return jnp.repeat(jnp.exp(heights), dims[axis_at] // shards_of).reshape((-1,) + (1,) * (len(dims) - axis_at - 1))

    loudness = one(*shards[0])
    for cut in shards[1:]:
        loudness = loudness * one(*cut)
    return loudness


def profile(number_of, total, bound, skew):
    portions = [(1 << 20) // math.isqrt(standing ** skew) + 1 for standing in range(2, number_of + 1)]
    spare, holding = total - bound - (number_of - 1), [1] * (number_of - 1)
    while spare > 0:
        free = [i for i in range(number_of - 1) if holding[i] < bound]
        pool, left = sum([portions[i] for i in free]), spare
        for i in free:
            addition = min(bound - holding[i], max(1, left * portions[i] // pool), spare)
            holding[i] = holding[i] + addition
            spare = spare - addition
    return np.array([bound] + holding)


def uneven(key, number_of, total, reach, slope):
    if number_of == 2:
        one = jax.random.randint(key, (), max(1, total - reach), min(reach, total - 1) + 1)
        return jnp.stack([one, total - one])
    lengths = jnp.asarray(profile(number_of, total, reach, slope), jnp.int32)
    twos = (number_of - 1) // 2
    giver, receiver = lengths[1:1 + 2 * twos:2], lengths[2:2 + 2 * twos:2]
    margin = jnp.minimum(giver - 1, reach - receiver)
    passed = jax.random.randint(jax.random.fold_in(key, 1), (twos,), 0, 1 << 20) % (margin + 1)
    lengths = lengths.at[1:1 + 2 * twos:2].set(giver - passed).at[2:2 + 2 * twos:2].set(receiver + passed)
    return lengths[jax.random.permutation(jax.random.fold_in(key, 2), number_of)]


def bell_draw(key, shape, scale, bound, pieces=(), held_as=jnp.bfloat16):
    drawn = jax.random.normal(key, shape, jnp.float32) * scale
    if len(pieces) > 0:
        drawn = block_scale(key, shape, pieces, -0.22, 0.18) * drawn
    return jnp.clip(drawn, min=-bound, max=bound).astype(held_as)


def setup_inputs(seed: int = 0) -> dict:
    splits = jax.random.split(jax.random.key(seed), 16)
    return {
        "prefill_tokens": bell_draw(splits[0], (PRE_TOKENS, D), 0.5, 3.0, ((0, 32),)),
        "decode_tokens": bell_draw(splits[1], (R_DEC, D), 0.5, 3.0, ((0, 32),)),
        "query_weight": bell_draw(splits[2], (D, D), D ** -0.5, 0.125, ((0, 32), (1, 8))),
        "key_weight": bell_draw(splits[3], (D, D), D ** -0.5, 0.125, ((0, 32), (1, 8))),
        "value_weight": bell_draw(splits[4], (D, D), D ** -0.5, 0.125, ((0, 32), (1, 8))),
        "out_weight": bell_draw(splits[5], (D, D), D ** -0.5, 0.125, ((0, 8), (1, 32))),
        "prior_keys": draw_prior_keys(jax.random.fold_in(splits[15], 71), 0),
        "prior_values": bell_draw(splits[7], (R_PRE, PRIOR_MAX, D), 1.0, 6.0, ((0, 32), (2, 8))),
        "prior_length": draw_prior_length(jax.random.fold_in(splits[15], 71), 0),
        "pool_keys": draw_pool_keys(jax.random.fold_in(splits[15], 71), 0),
        "pool_values": bell_draw(splits[10], (POOL, PAGE, D), 1.0, 6.0, ((0, 32), (2, 8))),
        "page_slots": jax.random.permutation(splits[11], POOL).astype(jnp.int32),
        "page_counts": uneven(splits[12], R_DEC, POOL, MAXP, 2).astype(jnp.int32),
        "last_fill": set_ends(jax.random.randint(splits[13], (R_DEC,), 1, PAGE + 1), jax.random.fold_in(splits[13], 1), 1, PAGE).astype(jnp.int32),
        "decode_request": jax.random.permutation(splits[14], R_DEC).astype(jnp.int32),
    }


EPSILON = 1e-05
ROPE_BASE = 10000.0
NEG_FILL = -1e+30

def layer_norm(rows_in):
    widened = rows_in.astype(jnp.float32)
    average = lax.optimization_barrier(jnp.mean(widened, axis=-1, keepdims=True))
    centred = widened - average
    variance = lax.optimization_barrier(jnp.mean(centred * centred, axis=-1, keepdims=True))
    return (centred * lax.rsqrt(variance + EPSILON)).astype(jnp.bfloat16)

def rotary(vectors, positions, head_size):
    row_count = vectors.shape[0]
    split_heads = vectors.reshape(row_count, -1, head_size)
    halfway = head_size // 2
    exponent = jnp.arange(halfway, dtype=jnp.float32) * (2.0 / head_size)
    frequency = jnp.power(jnp.float32(ROPE_BASE), -exponent)
    angles = positions.astype(jnp.float32)[:, None] * frequency[None, :]
    cosine = jnp.cos(angles)[:, None, :]
    sine_part = jnp.sin(angles)[:, None, :]
    leading = split_heads[..., :halfway]
    trailing = split_heads[..., halfway:]
    turned = jnp.concatenate([leading * cosine - trailing * sine_part, trailing * cosine + leading * sine_part], axis=-1)
    return turned.reshape(row_count, -1)

def reference(prefill_tokens, decode_tokens, query_weight, key_weight, value_weight, out_weight, prior_keys, prior_values, prior_length, pool_keys, pool_values, page_slots, page_counts, last_fill, decode_request):
    score_scale = HEAD ** (-0.5)
    tokens = jnp.concatenate([prefill_tokens, decode_tokens], axis=0)
    normed = layer_norm(tokens)
    raw_queries = jnp.dot(normed, query_weight, preferred_element_type=jnp.float32)
    raw_keys = jnp.dot(normed, key_weight, preferred_element_type=jnp.float32)
    raw_values = jnp.dot(normed, value_weight, preferred_element_type=jnp.float32)
    cache_length = ((page_counts - 1) * PAGE + last_fill).astype(jnp.int32)
    first_page = (jnp.cumsum(page_counts) - page_counts).astype(jnp.int32)
    group_offsets = jnp.tile(jnp.arange(GROUP, dtype=jnp.int32), R_PRE)
    prefill_positions = (jnp.repeat(prior_length, GROUP) + group_offsets).astype(jnp.int32)
    positions = jnp.concatenate([prefill_positions, jnp.take(cache_length, decode_request)])
    queries = lax.optimization_barrier(rotary(raw_queries, positions, HEAD).astype(jnp.bfloat16))
    keys_new = lax.optimization_barrier(rotary(raw_keys, positions, HEAD).astype(jnp.bfloat16))
    values_new = lax.optimization_barrier(raw_values.astype(jnp.bfloat16))
    prefill_rows = R_PRE * GROUP
    causal = jnp.arange(GROUP)[None, :] <= jnp.arange(GROUP)[:, None]

    def prefill_one(request):
        start_row = request * GROUP
        group_queries = lax.dynamic_slice_in_dim(queries, start_row, GROUP, 0).reshape(GROUP, HEADS, HEAD).astype(jnp.float32)
        group_keys = lax.dynamic_slice_in_dim(keys_new, start_row, GROUP, 0).reshape(GROUP, HEADS, HEAD).astype(jnp.float32)
        group_values = lax.dynamic_slice_in_dim(values_new, start_row, GROUP, 0).reshape(GROUP, HEADS, HEAD).astype(jnp.float32)
        stored_keys = lax.dynamic_index_in_dim(prior_keys, request, 0, keepdims=False).reshape(PRIOR_MAX, HEADS, HEAD).astype(jnp.float32)
        stored_values = lax.dynamic_index_in_dim(prior_values, request, 0, keepdims=False).reshape(PRIOR_MAX, HEADS, HEAD).astype(jnp.float32)
        prior_scores = jnp.einsum('qhd,khd->hqk', group_queries, stored_keys) * score_scale
        prior_live = jnp.arange(PRIOR_MAX, dtype=jnp.int32) < prior_length[request]
        prior_scores = jnp.where(prior_live[None, None, :], prior_scores, NEG_FILL)
        group_scores = jnp.einsum('qhd,khd->hqk', group_queries, group_keys) * score_scale
        group_scores = jnp.where(causal[None], group_scores, NEG_FILL)
        row_top = jnp.maximum(lax.optimization_barrier(jnp.max(prior_scores, axis=2, keepdims=True)), lax.optimization_barrier(jnp.max(group_scores, axis=2, keepdims=True)))
        prior_weights = jnp.exp(prior_scores - row_top)
        group_weights = jnp.exp(group_scores - row_top)
        weight_total = lax.optimization_barrier(jnp.sum(prior_weights, axis=2)) + lax.optimization_barrier(jnp.sum(group_weights, axis=2))
        prior_rounded = lax.optimization_barrier(prior_weights.astype(jnp.bfloat16)).astype(jnp.float32)
        group_rounded = lax.optimization_barrier(group_weights.astype(jnp.bfloat16)).astype(jnp.float32)
        combined = jnp.einsum('hqk,khd->qhd', prior_rounded, stored_values) + jnp.einsum('hqk,khd->qhd', group_rounded, group_values)
        attended = combined / jnp.transpose(weight_total)[:, :, None]
        return attended.reshape(GROUP, D).astype(jnp.bfloat16)
    prefill_attended = lax.map(prefill_one, jnp.arange(R_PRE, dtype=jnp.int32)).reshape(prefill_rows, D)

    def decode_one(slot):
        request = decode_request[slot]
        length = cache_length[request]
        logical = jnp.minimum(first_page[request] + jnp.arange(MAXP, dtype=jnp.int32), POOL - 1).astype(jnp.int32)
        slot_list = jnp.take(page_slots, logical)
        cached_keys = jnp.take(pool_keys, slot_list, axis=0).reshape(MAXP * PAGE, HEADS, HEAD).astype(jnp.float32)
        cached_values = jnp.take(pool_values, slot_list, axis=0).reshape(MAXP * PAGE, HEADS, HEAD).astype(jnp.float32)
        row_index = prefill_rows + slot
        own_query = lax.dynamic_index_in_dim(queries, row_index, 0, keepdims=False).reshape(HEADS, HEAD).astype(jnp.float32)
        own_key = lax.dynamic_index_in_dim(keys_new, row_index, 0, keepdims=False).reshape(HEADS, HEAD).astype(jnp.float32)
        own_value = lax.dynamic_index_in_dim(values_new, row_index, 0, keepdims=False).reshape(HEADS, HEAD).astype(jnp.float32)
        cache_scores = jnp.einsum('hd,khd->hk', own_query, cached_keys) * score_scale
        live = jnp.arange(MAXP * PAGE, dtype=jnp.int32) < length
        cache_scores = jnp.where(live[None, :], cache_scores, NEG_FILL)
        own_score = lax.optimization_barrier(jnp.sum(own_query * own_key, axis=1)) * score_scale
        row_top = jnp.maximum(lax.optimization_barrier(jnp.max(cache_scores, axis=1)), own_score)
        cache_weights = jnp.exp(cache_scores - row_top[:, None])
        own_weight = jnp.exp(own_score - row_top)
        weight_total = lax.optimization_barrier(jnp.sum(cache_weights, axis=1)) + own_weight
        combined = jnp.einsum('hk,khd->hd', cache_weights, cached_values) + own_weight[:, None] * own_value
        return (combined / weight_total[:, None]).reshape(D).astype(jnp.bfloat16)
    decode_attended = lax.map(decode_one, jnp.arange(R_DEC, dtype=jnp.int32))
    attended = jnp.concatenate([prefill_attended, decode_attended], axis=0)
    projected = jnp.dot(attended, out_weight, preferred_element_type=jnp.float32)
    mixed = (tokens.astype(jnp.float32) + projected).astype(jnp.bfloat16)
    return (mixed[:prefill_rows], mixed[prefill_rows:])
```

```python
import functools

import jax
import jax.numpy as jnp
from jax import lax
from jax.sharding import PartitionSpec as P

HEAD = 128
PAGE = 128


EPSILON = 1e-05
ROPE_BASE = 10000.0
NEG_FILL = -1e30


def layer_norm(rows_in):
    widened = rows_in.astype(jnp.float32)
    average = jnp.mean(widened, axis=-1, keepdims=True)
    centred = widened - average
    variance = jnp.mean(centred * centred, axis=-1, keepdims=True)
    return (centred * lax.rsqrt(variance + EPSILON)).astype(jnp.bfloat16)


def rotary(vectors, positions, head_size):
    row_count = vectors.shape[0]
    split_heads = vectors.reshape(row_count, -1, head_size)
    halfway = head_size // 2
    exponent = jnp.arange(halfway, dtype=jnp.float32) * (2.0 / head_size)
    frequency = jnp.power(jnp.float32(ROPE_BASE), -exponent)
    angles = positions.astype(jnp.float32)[:, None] * frequency[None, :]
    cosine = jnp.cos(angles)[:, None, :]
    sine_part = jnp.sin(angles)[:, None, :]
    leading = split_heads[..., :halfway]
    trailing = split_heads[..., halfway:]
    turned = jnp.concatenate(
        [leading * cosine - trailing * sine_part, trailing * cosine + leading * sine_part], axis=-1
    )
    return turned.reshape(row_count, -1)


def rescale(vectors, factor, head_size):
    shaped = vectors.reshape(vectors.shape[0], factor.shape[1], head_size)
    return (shaped * factor[:, :, None]).reshape(vectors.shape)


def inverse_permutation(order):
    count = order.shape[0]
    numbers = jnp.arange(count, dtype=jnp.int32)
    hit = order[None, :] == numbers[:, None]
    return jnp.sum(jnp.where(hit, numbers[None, :], 0), axis=1)


def per_device(
    prefill_tokens,
    decode_tokens,
    query_weight,
    key_weight,
    value_weight,
    out_weight,
    prior_keys,
    prior_values,
    prior_length,
    pool_keys,
    pool_values,
    page_slots,
    page_counts,
    last_fill,
    decode_request,
    *,
    dp_size,
):
    group_rows = prefill_tokens.shape[0]
    decode_rows = decode_tokens.shape[0]
    weight_rows = query_weight.shape[0]
    local_width = query_weight.shape[1]
    head_count = local_width // HEAD
    score_scale = HEAD ** (-0.5)
    data_index = lax.axis_index("dp")
    model_index = lax.axis_index("fsdp")

    projection_piece = jnp.concatenate([query_weight, key_weight, value_weight], axis=1)
    bundle_width = projection_piece.shape[1]
    out_size = out_weight.size
    tail = jnp.concatenate([out_weight.reshape(-1), decode_tokens.reshape(-1)])
    bundle = jnp.concatenate([projection_piece, tail.reshape(-1, bundle_width)], axis=0)
    gathered = lax.all_gather(bundle, "dp", axis=0, tiled=False)
    projection_weight = gathered[:, :weight_rows].reshape(-1, bundle_width)
    gathered_tail = gathered[:, weight_rows:].reshape(dp_size, -1)
    out_full = jnp.transpose(
        gathered_tail[:, :out_size].reshape(dp_size, out_weight.shape[0], out_weight.shape[1]),
        (1, 0, 2),
    ).reshape(out_weight.shape[0], -1)
    all_decode = gathered_tail[:, out_size:].reshape(dp_size * decode_rows, -1)

    tokens = jnp.concatenate([prefill_tokens, all_decode], axis=0)
    normed = layer_norm(tokens)
    raw = jnp.dot(normed, projection_weight, preferred_element_type=jnp.float32)
    raw_queries = raw[:, :local_width]
    raw_keys = raw[:, local_width : 2 * local_width]
    raw_values = raw[:, 2 * local_width :]

    cache_length = (page_counts - 1) * PAGE + last_fill
    first_page = jnp.cumsum(page_counts) - page_counts
    request_count = decode_request.shape[0]
    slot_numbers = jnp.arange(request_count, dtype=jnp.int32)
    slot_of_request = inverse_permutation(decode_request)
    positions = jnp.concatenate(
        [
            prior_length[0] + jnp.arange(group_rows, dtype=jnp.int32),
            jnp.take(cache_length, decode_request),
        ]
    )
    queries = rotary(raw_queries, positions, HEAD).astype(jnp.bfloat16)
    keys_new = rotary(raw_keys, positions, HEAD).astype(jnp.bfloat16)
    values_new = raw_values.astype(jnp.bfloat16)

    prior_slots = prior_keys.shape[1]
    group_queries = queries[:group_rows].reshape(group_rows, head_count, HEAD)
    group_keys = keys_new[:group_rows].reshape(group_rows, head_count, HEAD)
    group_values = values_new[:group_rows].reshape(group_rows, head_count, HEAD)
    stored_keys = prior_keys[0].reshape(prior_slots, head_count, HEAD)
    stored_values = prior_values[0].reshape(prior_slots, head_count, HEAD)
    prior_scores = (
        jnp.einsum("qhd,khd->hqk", group_queries, stored_keys, preferred_element_type=jnp.float32)
        * score_scale
    )
    prior_live = jnp.arange(prior_slots, dtype=jnp.int32) < prior_length[0]
    prior_scores = jnp.where(prior_live[None, None, :], prior_scores, NEG_FILL)
    group_scores = (
        jnp.einsum("qhd,khd->hqk", group_queries, group_keys, preferred_element_type=jnp.float32)
        * score_scale
    )
    causal = jnp.arange(group_rows)[None, :] <= jnp.arange(group_rows)[:, None]
    group_scores = jnp.where(causal[None], group_scores, NEG_FILL)
    row_top = jnp.maximum(
        jnp.max(prior_scores, axis=2, keepdims=True), jnp.max(group_scores, axis=2, keepdims=True)
    )
    prior_weights = jnp.exp(prior_scores - row_top)
    group_weights = jnp.exp(group_scores - row_top)
    weight_total = jnp.sum(prior_weights, axis=2) + jnp.sum(group_weights, axis=2)
    combined = jnp.einsum(
        "hqk,khd->qhd",
        prior_weights.astype(jnp.bfloat16),
        stored_values,
        preferred_element_type=jnp.float32,
    )
    combined = combined + jnp.einsum(
        "hqk,khd->qhd",
        group_weights.astype(jnp.bfloat16),
        group_values,
        preferred_element_type=jnp.float32,
    )
    prefill_attended = (
        (combined / jnp.transpose(weight_total)[:, :, None])
        .reshape(group_rows, local_width)
        .astype(jnp.bfloat16)
    )

    slot_queries = queries[group_rows:]
    own_start = data_index * decode_rows
    own_queries = lax.dynamic_slice_in_dim(slot_queries, own_start, decode_rows, 0)
    own_keys = lax.dynamic_slice_in_dim(keys_new[group_rows:], own_start, decode_rows, 0)
    own_values = lax.dynamic_slice_in_dim(values_new[group_rows:], own_start, decode_rows, 0)
    pool_count = page_slots.shape[0]
    pool_local = pool_keys.shape[0]
    local_slots = data_index * pool_local + jnp.arange(pool_local, dtype=jnp.int32)
    slot_hit = page_slots[None, :] == local_slots[:, None]
    local_logical = jnp.sum(
        jnp.where(slot_hit, jnp.arange(pool_count, dtype=jnp.int32)[None, :], 0), axis=1
    )
    page_owner = (
        jnp.sum((first_page[None, :] <= local_logical[:, None]).astype(jnp.int32), axis=1) - 1
    )
    page_number = local_logical - jnp.take(first_page, page_owner)
    page_slot = jnp.take(slot_of_request, page_owner)
    page_queries = jnp.take(slot_queries, page_slot, axis=0).reshape(pool_local, head_count, HEAD)
    page_keys = pool_keys.reshape(pool_local, PAGE, head_count, HEAD)
    page_scores = (
        jnp.einsum("phd,pkhd->phk", page_queries, page_keys, preferred_element_type=jnp.float32)
        * score_scale
    )
    key_place = page_number[:, None] * PAGE + jnp.arange(PAGE, dtype=jnp.int32)[None, :]
    page_live = key_place < jnp.take(cache_length, page_owner)[:, None]
    page_scores = jnp.where(page_live[:, None, :], page_scores, NEG_FILL)
    member = page_slot[:, None] == slot_numbers[None, :]
    page_top = jnp.max(page_scores, axis=2)
    local_top = jnp.max(jnp.where(member[:, :, None], page_top[:, None, :], NEG_FILL), axis=0)
    slot_top = lax.pmax(local_top, "dp")
    page_weights = jnp.exp(page_scores - jnp.take(slot_top, page_slot, axis=0)[:, :, None])
    member_weights = member.astype(jnp.float32)
    slot_total = jnp.dot(
        member_weights.T, jnp.sum(page_weights, axis=2), precision=lax.Precision.HIGHEST
    )
    page_values = pool_values.reshape(pool_local, PAGE, head_count, HEAD).astype(jnp.float32)
    page_mix = jnp.einsum(
        "phk,pkhd->phd", page_weights, page_values, precision=lax.Precision.HIGHEST
    )
    slot_mix = jnp.dot(
        member_weights.T, page_mix.reshape(pool_local, local_width), precision=lax.Precision.HIGHEST
    )
    partials = jnp.concatenate([slot_total, slot_mix], axis=1)
    mine = lax.psum_scatter(partials, "dp", scatter_dimension=0, tiled=True)
    mine_total = mine[:, :head_count]
    mine_mix = mine[:, head_count:]
    mine_top = lax.dynamic_slice_in_dim(slot_top, own_start, decode_rows, 0)
    own_score = (
        jnp.einsum(
            "rhd,rhd->rh",
            own_queries.reshape(decode_rows, head_count, HEAD),
            own_keys.reshape(decode_rows, head_count, HEAD),
            preferred_element_type=jnp.float32,
        )
        * score_scale
    )
    final_top = jnp.maximum(mine_top, own_score)
    cache_factor = jnp.exp(mine_top - final_top)
    own_factor = jnp.exp(own_score - final_top)
    final_total = mine_total * cache_factor + own_factor
    final_mix = rescale(mine_mix, cache_factor, HEAD) + rescale(
        own_values.astype(jnp.float32), own_factor, HEAD
    )
    decode_attended = rescale(final_mix, 1.0 / final_total, HEAD).astype(jnp.bfloat16)
    attended = jnp.concatenate([prefill_attended, decode_attended], axis=0)
    own_tokens = jnp.concatenate([prefill_tokens, decode_tokens], axis=0)
    residual = lax.dynamic_slice_in_dim(own_tokens, model_index * local_width, local_width, 1)
    terms = jnp.dot(attended, out_full, preferred_element_type=jnp.float32)
    branch = lax.psum_scatter(
        terms.astype(jnp.bfloat16), "fsdp", scatter_dimension=1, tiled=True
    ).astype(jnp.float32)
    result = (residual.astype(jnp.float32) + branch).astype(jnp.bfloat16)
    return (result[:group_rows], result[group_rows:])


def solution(mesh):
    in_specs = (
        P("dp", None),
        P("dp", None),
        P("dp", "fsdp"),
        P("dp", "fsdp"),
        P("dp", "fsdp"),
        P("fsdp", "dp"),
        P("dp", None, "fsdp"),
        P("dp", None, "fsdp"),
        P("dp"),
        P("dp", None, "fsdp"),
        P("dp", None, "fsdp"),
        P(),
        P(),
        P(),
        P(),
    )
    out_specs = (P("dp", "fsdp"), P("dp", "fsdp"))
    return jax.shard_map(
        functools.partial(per_device, dp_size=mesh.shape["dp"]),
        mesh=mesh,
        in_specs=in_specs,
        out_specs=out_specs,
        check_vma=False,
    )
```

```python
import functools

import jax
import jax.numpy as jnp
from jax import lax
from jax.sharding import PartitionSpec as P

HEAD = 128
PAGE = 128


EPSILON = 1e-05
ROPE_BASE = 10000.0
NEG_FILL = -1e30


def layer_norm(rows_in):
    widened = rows_in.astype(jnp.float32)
    average = jnp.mean(widened, axis=-1, keepdims=True)
    centred = widened - average
    variance = jnp.mean(centred * centred, axis=-1, keepdims=True)
    return (centred * lax.rsqrt(variance + EPSILON)).astype(jnp.bfloat16)


def rotary(vectors, positions, head_size):
    row_count = vectors.shape[0]
    split_heads = vectors.reshape(row_count, -1, head_size)
    halfway = head_size // 2
    exponent = jnp.arange(halfway, dtype=jnp.float32) * (2.0 / head_size)
    frequency = jnp.power(jnp.float32(ROPE_BASE), -exponent)
    angles = positions.astype(jnp.float32)[:, None] * frequency[None, :]
    cosine = jnp.cos(angles)[:, None, :]
    sine_part = jnp.sin(angles)[:, None, :]
    leading = split_heads[..., :halfway]
    trailing = split_heads[..., halfway:]
    turned = jnp.concatenate(
        [leading * cosine - trailing * sine_part, trailing * cosine + leading * sine_part], axis=-1
    )
    return turned.reshape(row_count, -1)


def rescale(vectors, factor, head_size):
    shaped = vectors.reshape(vectors.shape[0], factor.shape[1], head_size)
    return (shaped * factor[:, :, None]).reshape(vectors.shape)


def inverse_permutation(order):
    count = order.shape[0]
    numbers = jnp.arange(count, dtype=jnp.int32)
    hit = order[None, :] == numbers[:, None]
    return jnp.sum(jnp.where(hit, numbers[None, :], 0), axis=1)


def per_device(
    prefill_tokens,
    decode_tokens,
    query_weight,
    key_weight,
    value_weight,
    out_weight,
    prior_keys,
    prior_values,
    prior_length,
    pool_keys,
    pool_values,
    page_slots,
    page_counts,
    last_fill,
    decode_request,
    *,
    dp_size,
):
    group_rows = prefill_tokens.shape[0]
    decode_rows = decode_tokens.shape[0]
    weight_rows = query_weight.shape[0]
    local_width = query_weight.shape[1]
    head_count = local_width // HEAD
    score_scale = HEAD ** (-0.5)
    data_index = lax.axis_index("dp")
    model_index = lax.axis_index("fsdp")

    projection_piece = jnp.concatenate([query_weight, key_weight, value_weight], axis=1)
    bundle_width = projection_piece.shape[1]
    out_size = out_weight.size
    tail = jnp.concatenate([out_weight.reshape(-1), decode_tokens.reshape(-1)])
    bundle = jnp.concatenate([projection_piece, tail.reshape(-1, bundle_width)], axis=0)
    gathered = lax.all_gather(bundle, "dp", axis=0, tiled=False)
    projection_weight = gathered[:, :weight_rows].reshape(-1, bundle_width)
    gathered_tail = gathered[:, weight_rows:].reshape(dp_size, -1)
    out_full = jnp.transpose(
        gathered_tail[:, :out_size].reshape(dp_size, out_weight.shape[0], out_weight.shape[1]),
        (1, 0, 2),
    ).reshape(out_weight.shape[0], -1)
    all_decode = gathered_tail[:, out_size:].reshape(dp_size * decode_rows, -1)

    tokens = jnp.concatenate([prefill_tokens, all_decode], axis=0)
    normed = layer_norm(tokens)
    raw = jnp.dot(normed, projection_weight, preferred_element_type=jnp.float32)
    raw_queries = raw[:, :local_width]
    raw_keys = raw[:, local_width : 2 * local_width]
    raw_values = raw[:, 2 * local_width :]

    cache_length = (page_counts - 1) * PAGE + last_fill
    first_page = jnp.cumsum(page_counts) - page_counts
    request_count = decode_request.shape[0]
    slot_numbers = jnp.arange(request_count, dtype=jnp.int32)
    slot_of_request = inverse_permutation(decode_request)
    positions = jnp.concatenate(
        [
            prior_length[0] + jnp.arange(group_rows, dtype=jnp.int32),
            jnp.take(cache_length, decode_request),
        ]
    )
    queries = rotary(raw_queries, positions, HEAD).astype(jnp.bfloat16)
    keys_new = rotary(raw_keys, positions, HEAD).astype(jnp.bfloat16)
    values_new = raw_values.astype(jnp.bfloat16)

    prior_slots = prior_keys.shape[1]
    group_queries = queries[:group_rows].reshape(group_rows, head_count, HEAD)
    group_keys = keys_new[:group_rows].reshape(group_rows, head_count, HEAD)
    group_values = values_new[:group_rows].reshape(group_rows, head_count, HEAD)
    stored_keys = prior_keys[0].reshape(prior_slots, head_count, HEAD)
    stored_values = prior_values[0].reshape(prior_slots, head_count, HEAD)
    prior_scores = (
        jnp.einsum("qhd,khd->hqk", group_queries, stored_keys, preferred_element_type=jnp.float32)
        * score_scale
    )
    prior_live = jnp.arange(prior_slots, dtype=jnp.int32) < prior_length[0]
    prior_scores = jnp.where(prior_live[None, None, :], prior_scores, NEG_FILL)
    group_scores = (
        jnp.einsum("qhd,khd->hqk", group_queries, group_keys, preferred_element_type=jnp.float32)
        * score_scale
    )
    causal = jnp.arange(group_rows)[None, :] <= jnp.arange(group_rows)[:, None]
    group_scores = jnp.where(causal[None], group_scores, NEG_FILL)
    row_top = jnp.maximum(
        jnp.max(prior_scores, axis=2, keepdims=True), jnp.max(group_scores, axis=2, keepdims=True)
    )
    prior_weights = jnp.exp(prior_scores - row_top)
    group_weights = jnp.exp(group_scores - row_top)
    weight_total = jnp.sum(prior_weights, axis=2) + jnp.sum(group_weights, axis=2)
    combined = jnp.einsum(
        "hqk,khd->qhd",
        prior_weights.astype(jnp.bfloat16),
        stored_values,
        preferred_element_type=jnp.float32,
    )
    combined = combined + jnp.einsum(
        "hqk,khd->qhd",
        group_weights.astype(jnp.bfloat16),
        group_values,
        preferred_element_type=jnp.float32,
    )
    prefill_attended = (
        (combined / jnp.transpose(weight_total)[:, :, None])
        .reshape(group_rows, local_width)
        .astype(jnp.bfloat16)
    )

    slot_queries = queries[group_rows:]
    own_start = data_index * decode_rows
    own_queries = lax.dynamic_slice_in_dim(slot_queries, own_start, decode_rows, 0)
    own_keys = lax.dynamic_slice_in_dim(keys_new[group_rows:], own_start, decode_rows, 0)
    own_values = lax.dynamic_slice_in_dim(values_new[group_rows:], own_start, decode_rows, 0)
    pool_count = page_slots.shape[0]
    pool_local = pool_keys.shape[0]
    local_slots = data_index * pool_local + jnp.arange(pool_local, dtype=jnp.int32)
    slot_hit = page_slots[None, :] == local_slots[:, None]
    local_logical = jnp.sum(
        jnp.where(slot_hit, jnp.arange(pool_count, dtype=jnp.int32)[None, :], 0), axis=1
    )
    page_owner = (
        jnp.sum((first_page[None, :] <= local_logical[:, None]).astype(jnp.int32), axis=1) - 1
    )
    page_number = local_logical - jnp.take(first_page, page_owner)
    page_slot = jnp.take(slot_of_request, page_owner)
    page_queries = jnp.take(slot_queries, page_slot, axis=0).reshape(pool_local, head_count, HEAD)
    page_keys = pool_keys.reshape(pool_local, PAGE, head_count, HEAD)
    page_scores = (
        jnp.einsum("phd,pkhd->phk", page_queries, page_keys, preferred_element_type=jnp.float32)
        * score_scale
    )
    key_place = page_number[:, None] * PAGE + jnp.arange(PAGE, dtype=jnp.int32)[None, :]
    page_live = key_place < jnp.take(cache_length, page_owner)[:, None]
    page_scores = jnp.where(page_live[:, None, :], page_scores, NEG_FILL)
    member = page_slot[:, None] == slot_numbers[None, :]
    page_top = jnp.max(page_scores, axis=2)
    slot_top = jnp.max(jnp.where(member[:, :, None], page_top[:, None, :], NEG_FILL), axis=0)
    page_weights = jnp.exp(page_scores - jnp.take(slot_top, page_slot, axis=0)[:, :, None])
    member_weights = member.astype(jnp.float32)
    slot_total = jnp.dot(
        member_weights.T, jnp.sum(page_weights, axis=2), precision=lax.Precision.HIGHEST
    )
    page_values = pool_values.reshape(pool_local, PAGE, head_count, HEAD).astype(jnp.float32)
    page_mix = jnp.einsum(
        "phk,pkhd->phd", page_weights, page_values, precision=lax.Precision.HIGHEST
    )
    slot_mix = jnp.dot(
        member_weights.T, page_mix.reshape(pool_local, local_width), precision=lax.Precision.HIGHEST
    )
    partials = jnp.concatenate([slot_top, slot_total, slot_mix], axis=1)
    received = lax.all_to_all(
        partials.reshape(dp_size, decode_rows, -1), "dp", 0, 0, tiled=False
    )
    source_top = received[:, :, :head_count]
    source_total = received[:, :, head_count : 2 * head_count]
    source_mix = received[:, :, 2 * head_count :]
    mine_top = jnp.max(source_top, axis=0)
    source_factor = jnp.exp(source_top - mine_top[None])
    mine_total = jnp.sum(source_total * source_factor, axis=0)
    mine_mix = jnp.sum(
        source_mix.reshape(dp_size, decode_rows, head_count, HEAD) * source_factor[..., None], axis=0
    ).reshape(decode_rows, local_width)
    own_score = (
        jnp.einsum(
            "rhd,rhd->rh",
            own_queries.reshape(decode_rows, head_count, HEAD),
            own_keys.reshape(decode_rows, head_count, HEAD),
            preferred_element_type=jnp.float32,
        )
        * score_scale
    )
    final_top = jnp.maximum(mine_top, own_score)
    cache_factor = jnp.exp(mine_top - final_top)
    own_factor = jnp.exp(own_score - final_top)
    final_total = mine_total * cache_factor + own_factor
    final_mix = rescale(mine_mix, cache_factor, HEAD) + rescale(
        own_values.astype(jnp.float32), own_factor, HEAD
    )
    decode_attended = rescale(final_mix, 1.0 / final_total, HEAD).astype(jnp.bfloat16)
    attended = jnp.concatenate([prefill_attended, decode_attended], axis=0)
    own_tokens = jnp.concatenate([prefill_tokens, decode_tokens], axis=0)
    residual = lax.dynamic_slice_in_dim(own_tokens, model_index * local_width, local_width, 1)
    terms = jnp.dot(attended, out_full, preferred_element_type=jnp.float32).astype(jnp.bfloat16)
    model_size = terms.shape[1] // local_width
    shares = jnp.transpose(terms.reshape(terms.shape[0], model_size, local_width), (1, 0, 2))
    branch = jnp.sum(
        lax.all_to_all(shares, "fsdp", 0, 0, tiled=False).astype(jnp.float32), axis=0
    )
    result = (residual.astype(jnp.float32) + branch).astype(jnp.bfloat16)
    return (result[:group_rows], result[group_rows:])


def solution(mesh):
    in_specs = (
        P("dp", None),
        P("dp", None),
        P("dp", "fsdp"),
        P("dp", "fsdp"),
        P("dp", "fsdp"),
        P("fsdp", "dp"),
        P("dp", None, "fsdp"),
        P("dp", None, "fsdp"),
        P("dp"),
        P("dp", None, "fsdp"),
        P("dp", None, "fsdp"),
        P(),
        P(),
        P(),
        P(),
    )
    out_specs = (P("dp", "fsdp"), P("dp", "fsdp"))
    return jax.shard_map(
        functools.partial(per_device, dp_size=mesh.shape["dp"]),
        mesh=mesh,
        in_specs=in_specs,
        out_specs=out_specs,
        check_vma=False,
    )
```

```python
import functools

import jax
import jax.numpy as jnp
from jax import lax
from jax.sharding import PartitionSpec as P

HEAD = 128
PAGE = 128


EPSILON = 1e-05
ROPE_BASE = 10000.0
NEG_FILL = -1e30


def layer_norm(rows_in):
    widened = rows_in.astype(jnp.float32)
    average = jnp.mean(widened, axis=-1, keepdims=True)
    centred = widened - average
    variance = jnp.mean(centred * centred, axis=-1, keepdims=True)
    return (centred * lax.rsqrt(variance + EPSILON)).astype(jnp.bfloat16)


def rotary(vectors, positions, head_size):
    row_count = vectors.shape[0]
    split_heads = vectors.reshape(row_count, -1, head_size)
    halfway = head_size // 2
    exponent = jnp.arange(halfway, dtype=jnp.float32) * (2.0 / head_size)
    frequency = jnp.power(jnp.float32(ROPE_BASE), -exponent)
    angles = positions.astype(jnp.float32)[:, None] * frequency[None, :]
    cosine = jnp.cos(angles)[:, None, :]
    sine_part = jnp.sin(angles)[:, None, :]
    leading = split_heads[..., :halfway]
    trailing = split_heads[..., halfway:]
    turned = jnp.concatenate(
        [leading * cosine - trailing * sine_part, trailing * cosine + leading * sine_part], axis=-1
    )
    return turned.reshape(row_count, -1)


def rescale(vectors, factor, head_size):
    shaped = vectors.reshape(vectors.shape[0], factor.shape[1], head_size)
    return (shaped * factor[:, :, None]).reshape(vectors.shape)


def inverse_permutation(order):
    count = order.shape[0]
    numbers = jnp.arange(count, dtype=jnp.int32)
    hit = order[None, :] == numbers[:, None]
    return jnp.sum(jnp.where(hit, numbers[None, :], 0), axis=1)


def per_device(
    prefill_tokens,
    decode_tokens,
    query_weight,
    key_weight,
    value_weight,
    out_weight,
    prior_keys,
    prior_values,
    prior_length,
    pool_keys,
    pool_values,
    page_slots,
    page_counts,
    last_fill,
    decode_request,
    *,
    dp_size,
):
    group_rows = prefill_tokens.shape[0]
    decode_rows = decode_tokens.shape[0]
    weight_rows = query_weight.shape[0]
    local_width = query_weight.shape[1]
    head_count = local_width // HEAD
    score_scale = HEAD ** (-0.5)
    data_index = lax.axis_index("dp")
    model_index = lax.axis_index("fsdp")

    projection_piece = jnp.concatenate([query_weight, key_weight, value_weight], axis=1)
    projection_weight = lax.all_gather(projection_piece, "dp", axis=0, tiled=True)
    out_size = out_weight.size
    late_piece = jnp.concatenate([decode_tokens.reshape(-1), out_weight.reshape(-1)])
    projection_weight, late_piece = lax.optimization_barrier((projection_weight, late_piece))
    late = lax.all_gather(late_piece.reshape(-1, local_width), "dp", axis=0, tiled=False)
    late = late.reshape(dp_size, -1)
    decode_size = decode_tokens.size
    all_decode = late[:, :decode_size].reshape(dp_size * decode_rows, -1)
    out_full = jnp.transpose(
        late[:, decode_size:].reshape(dp_size, out_weight.shape[0], out_weight.shape[1]),
        (1, 0, 2),
    ).reshape(out_weight.shape[0], -1)

    def project(rows_in):
        raw = jnp.dot(layer_norm(rows_in), projection_weight, preferred_element_type=jnp.float32)
        return raw[:, :local_width], raw[:, local_width : 2 * local_width], raw[:, 2 * local_width :]

    cache_length = (page_counts - 1) * PAGE + last_fill
    first_page = jnp.cumsum(page_counts) - page_counts
    request_count = decode_request.shape[0]
    slot_numbers = jnp.arange(request_count, dtype=jnp.int32)
    slot_of_request = inverse_permutation(decode_request)
    prefill_q, prefill_k, prefill_v = project(prefill_tokens)
    prefill_positions = prior_length[0] + jnp.arange(group_rows, dtype=jnp.int32)
    decode_positions = jnp.take(cache_length, decode_request)
    group_queries = rotary(prefill_q, prefill_positions, HEAD).astype(jnp.bfloat16)
    group_keys = rotary(prefill_k, prefill_positions, HEAD).astype(jnp.bfloat16)
    group_values = prefill_v.astype(jnp.bfloat16)

    prior_slots = prior_keys.shape[1]
    group_queries = group_queries.reshape(group_rows, head_count, HEAD)
    group_keys = group_keys.reshape(group_rows, head_count, HEAD)
    group_values = group_values.reshape(group_rows, head_count, HEAD)
    stored_keys = prior_keys[0].reshape(prior_slots, head_count, HEAD)
    stored_values = prior_values[0].reshape(prior_slots, head_count, HEAD)
    prior_scores = (
        jnp.einsum("qhd,khd->hqk", group_queries, stored_keys, preferred_element_type=jnp.float32)
        * score_scale
    )
    prior_live = jnp.arange(prior_slots, dtype=jnp.int32) < prior_length[0]
    prior_scores = jnp.where(prior_live[None, None, :], prior_scores, NEG_FILL)
    group_scores = (
        jnp.einsum("qhd,khd->hqk", group_queries, group_keys, preferred_element_type=jnp.float32)
        * score_scale
    )
    causal = jnp.arange(group_rows)[None, :] <= jnp.arange(group_rows)[:, None]
    group_scores = jnp.where(causal[None], group_scores, NEG_FILL)
    row_top = jnp.maximum(
        jnp.max(prior_scores, axis=2, keepdims=True), jnp.max(group_scores, axis=2, keepdims=True)
    )
    prior_weights = jnp.exp(prior_scores - row_top)
    group_weights = jnp.exp(group_scores - row_top)
    weight_total = jnp.sum(prior_weights, axis=2) + jnp.sum(group_weights, axis=2)
    combined = jnp.einsum(
        "hqk,khd->qhd",
        prior_weights.astype(jnp.bfloat16),
        stored_values,
        preferred_element_type=jnp.float32,
    )
    combined = combined + jnp.einsum(
        "hqk,khd->qhd",
        group_weights.astype(jnp.bfloat16),
        group_values,
        preferred_element_type=jnp.float32,
    )
    prefill_attended = (
        (combined / jnp.transpose(weight_total)[:, :, None])
        .reshape(group_rows, local_width)
        .astype(jnp.bfloat16)
    )

    model_size = out_full.shape[1] // local_width
    column_start = model_index * local_width

    def send_shares(attended):
        terms = jnp.dot(attended, out_full, preferred_element_type=jnp.float32).astype(jnp.bfloat16)
        return jnp.transpose(terms.reshape(terms.shape[0], model_size, local_width), (1, 0, 2))

    def exchange(shares):
        return lax.all_to_all(shares, "fsdp", 0, 0, tiled=False)

    def mixed(received, own_tokens):
        branch = jnp.sum(received.astype(jnp.float32), axis=0)
        residual = lax.dynamic_slice_in_dim(own_tokens, column_start, local_width, 1)
        return (residual.astype(jnp.float32) + branch).astype(jnp.bfloat16)

    prefill_shares, all_decode = lax.optimization_barrier(
        (send_shares(prefill_attended), all_decode)
    )
    prefill_received = exchange(prefill_shares)
    decode_q, decode_k, decode_v = project(all_decode)
    slot_queries = rotary(decode_q, decode_positions, HEAD).astype(jnp.bfloat16)
    slot_keys = rotary(decode_k, decode_positions, HEAD).astype(jnp.bfloat16)
    slot_values = decode_v.astype(jnp.bfloat16)
    own_start = data_index * decode_rows
    own_queries = lax.dynamic_slice_in_dim(slot_queries, own_start, decode_rows, 0)
    own_keys = lax.dynamic_slice_in_dim(slot_keys, own_start, decode_rows, 0)
    own_values = lax.dynamic_slice_in_dim(slot_values, own_start, decode_rows, 0)
    pool_count = page_slots.shape[0]
    pool_local = pool_keys.shape[0]
    local_slots = data_index * pool_local + jnp.arange(pool_local, dtype=jnp.int32)
    slot_hit = page_slots[None, :] == local_slots[:, None]
    local_logical = jnp.sum(
        jnp.where(slot_hit, jnp.arange(pool_count, dtype=jnp.int32)[None, :], 0), axis=1
    )
    page_owner = (
        jnp.sum((first_page[None, :] <= local_logical[:, None]).astype(jnp.int32), axis=1) - 1
    )
    page_number = local_logical - jnp.take(first_page, page_owner)
    page_slot = jnp.take(slot_of_request, page_owner)
    page_queries = jnp.take(slot_queries, page_slot, axis=0).reshape(pool_local, head_count, HEAD)
    page_keys = pool_keys.reshape(pool_local, PAGE, head_count, HEAD)
    page_scores = (
        jnp.einsum("phd,pkhd->phk", page_queries, page_keys, preferred_element_type=jnp.float32)
        * score_scale
    )
    key_place = page_number[:, None] * PAGE + jnp.arange(PAGE, dtype=jnp.int32)[None, :]
    page_live = key_place < jnp.take(cache_length, page_owner)[:, None]
    page_scores = jnp.where(page_live[:, None, :], page_scores, NEG_FILL)
    member = page_slot[:, None] == slot_numbers[None, :]
    page_top = jnp.max(page_scores, axis=2)
    slot_top = jnp.max(jnp.where(member[:, :, None], page_top[:, None, :], NEG_FILL), axis=0)
    page_weights = jnp.exp(page_scores - jnp.take(slot_top, page_slot, axis=0)[:, :, None])
    member_weights = member.astype(jnp.float32)
    slot_total = jnp.dot(
        member_weights.T, jnp.sum(page_weights, axis=2), precision=lax.Precision.HIGHEST
    )
    page_values = pool_values.reshape(pool_local, PAGE, head_count, HEAD).astype(jnp.float32)
    page_mix = jnp.einsum(
        "phk,pkhd->phd", page_weights, page_values, precision=lax.Precision.HIGHEST
    )
    slot_mix = jnp.dot(
        member_weights.T, page_mix.reshape(pool_local, local_width), precision=lax.Precision.HIGHEST
    )
    partials = jnp.concatenate([slot_top, slot_total, slot_mix], axis=1)
    partials, prefill_received = lax.optimization_barrier((partials, prefill_received))
    received = lax.all_to_all(
        partials.reshape(dp_size, decode_rows, -1), "dp", 0, 0, tiled=False
    )
    source_top = received[:, :, :head_count]
    source_total = received[:, :, head_count : 2 * head_count]
    source_mix = received[:, :, 2 * head_count :]
    mine_top = jnp.max(source_top, axis=0)
    source_factor = jnp.exp(source_top - mine_top[None])
    mine_total = jnp.sum(source_total * source_factor, axis=0)
    mine_mix = jnp.sum(
        source_mix.reshape(dp_size, decode_rows, head_count, HEAD) * source_factor[..., None], axis=0
    ).reshape(decode_rows, local_width)
    own_score = (
        jnp.einsum(
            "rhd,rhd->rh",
            own_queries.reshape(decode_rows, head_count, HEAD),
            own_keys.reshape(decode_rows, head_count, HEAD),
            preferred_element_type=jnp.float32,
        )
        * score_scale
    )
    final_top = jnp.maximum(mine_top, own_score)
    cache_factor = jnp.exp(mine_top - final_top)
    own_factor = jnp.exp(own_score - final_top)
    final_total = mine_total * cache_factor + own_factor
    final_mix = rescale(mine_mix, cache_factor, HEAD) + rescale(
        own_values.astype(jnp.float32), own_factor, HEAD
    )
    decode_attended = rescale(final_mix, 1.0 / final_total, HEAD).astype(jnp.bfloat16)
    return (
        mixed(prefill_received, prefill_tokens),
        mixed(exchange(send_shares(decode_attended)), decode_tokens),
    )


def solution(mesh):
    in_specs = (
        P("dp", None),
        P("dp", None),
        P("dp", "fsdp"),
        P("dp", "fsdp"),
        P("dp", "fsdp"),
        P("fsdp", "dp"),
        P("dp", None, "fsdp"),
        P("dp", None, "fsdp"),
        P("dp"),
        P("dp", None, "fsdp"),
        P("dp", None, "fsdp"),
        P(),
        P(),
        P(),
        P(),
    )
    out_specs = (P("dp", "fsdp"), P("dp", "fsdp"))
    return jax.shard_map(
        functools.partial(per_device, dp_size=mesh.shape["dp"]),
        mesh=mesh,
        in_specs=in_specs,
        out_specs=out_specs,
        check_vma=False,
    )
```

```python
import functools

import jax
import jax.numpy as jnp
from jax import lax
from jax.sharding import PartitionSpec as P

HEAD = 128
PAGE = 128


EPSILON = 1e-05
ROPE_BASE = 10000.0
NEG_FILL = -1e30


def layer_norm(rows_in):
    widened = rows_in.astype(jnp.float32)
    average = jnp.mean(widened, axis=-1, keepdims=True)
    centred = widened - average
    variance = jnp.mean(centred * centred, axis=-1, keepdims=True)
    return (centred * lax.rsqrt(variance + EPSILON)).astype(jnp.bfloat16)


def rotary(vectors, positions, head_size):
    row_count = vectors.shape[0]
    split_heads = vectors.reshape(row_count, -1, head_size)
    halfway = head_size // 2
    exponent = jnp.arange(halfway, dtype=jnp.float32) * (2.0 / head_size)
    frequency = jnp.power(jnp.float32(ROPE_BASE), -exponent)
    angles = positions.astype(jnp.float32)[:, None] * frequency[None, :]
    cosine = jnp.cos(angles)[:, None, :]
    sine_part = jnp.sin(angles)[:, None, :]
    leading = split_heads[..., :halfway]
    trailing = split_heads[..., halfway:]
    turned = jnp.concatenate(
        [leading * cosine - trailing * sine_part, trailing * cosine + leading * sine_part], axis=-1
    )
    return turned.reshape(row_count, -1)


def rescale(vectors, factor, head_size):
    shaped = vectors.reshape(vectors.shape[0], factor.shape[1], head_size)
    return (shaped * factor[:, :, None]).reshape(vectors.shape)


def inverse_permutation(order):
    count = order.shape[0]
    numbers = jnp.arange(count, dtype=jnp.int32)
    hit = order[None, :] == numbers[:, None]
    return jnp.sum(jnp.where(hit, numbers[None, :], 0), axis=1)


def per_device(
    prefill_tokens,
    decode_tokens,
    query_weight,
    key_weight,
    value_weight,
    out_weight,
    prior_keys,
    prior_values,
    prior_length,
    pool_keys,
    pool_values,
    page_slots,
    page_counts,
    last_fill,
    decode_request,
    *,
    dp_size,
):
    group_rows = prefill_tokens.shape[0]
    decode_rows = decode_tokens.shape[0]
    weight_rows = query_weight.shape[0]
    local_width = query_weight.shape[1]
    head_count = local_width // HEAD
    score_scale = HEAD ** (-0.5)
    data_index = lax.axis_index("dp")
    model_index = lax.axis_index("fsdp")

    decode_piece = decode_tokens.reshape(-1, local_width)
    decode_piece = jnp.pad(decode_piece, ((0, weight_rows - decode_piece.shape[0]), (0, 0)))
    bundle = jnp.stack(
        [query_weight, key_weight, value_weight, jnp.transpose(out_weight), decode_piece]
    )
    gathered = lax.all_gather(bundle, "dp", axis=1, tiled=False)
    projection_weights = [gathered[p].reshape(-1, local_width) for p in range(3)]
    out_columns = gathered[3].reshape(-1, local_width)
    decode_size = decode_tokens.size
    all_decode = (
        gathered[4].reshape(dp_size, -1)[:, :decode_size].reshape(dp_size * decode_rows, -1)
    )

    def project(rows_in):
        normed = layer_norm(rows_in)
        return tuple(
            jnp.dot(normed, weight, preferred_element_type=jnp.float32)
            for weight in projection_weights
        )

    cache_length = (page_counts - 1) * PAGE + last_fill
    first_page = jnp.cumsum(page_counts) - page_counts
    request_count = decode_request.shape[0]
    slot_numbers = jnp.arange(request_count, dtype=jnp.int32)
    slot_of_request = inverse_permutation(decode_request)
    prefill_q, prefill_k, prefill_v = project(prefill_tokens)
    prefill_positions = prior_length[0] + jnp.arange(group_rows, dtype=jnp.int32)
    decode_positions = jnp.take(cache_length, decode_request)
    group_queries = rotary(prefill_q, prefill_positions, HEAD).astype(jnp.bfloat16)
    group_keys = rotary(prefill_k, prefill_positions, HEAD).astype(jnp.bfloat16)
    group_values = prefill_v.astype(jnp.bfloat16)

    prior_slots = prior_keys.shape[1]
    group_queries = group_queries.reshape(group_rows, head_count, HEAD)
    group_keys = group_keys.reshape(group_rows, head_count, HEAD)
    group_values = group_values.reshape(group_rows, head_count, HEAD)
    stored_keys = prior_keys[0].reshape(prior_slots, head_count, HEAD)
    stored_values = prior_values[0].reshape(prior_slots, head_count, HEAD)
    prior_scores = (
        jnp.einsum("qhd,khd->hqk", group_queries, stored_keys, preferred_element_type=jnp.float32)
        * score_scale
    )
    prior_live = jnp.arange(prior_slots, dtype=jnp.int32) < prior_length[0]
    prior_scores = jnp.where(prior_live[None, None, :], prior_scores, NEG_FILL)
    group_scores = (
        jnp.einsum("qhd,khd->hqk", group_queries, group_keys, preferred_element_type=jnp.float32)
        * score_scale
    )
    causal = jnp.arange(group_rows)[None, :] <= jnp.arange(group_rows)[:, None]
    group_scores = jnp.where(causal[None], group_scores, NEG_FILL)
    row_top = jnp.maximum(
        jnp.max(prior_scores, axis=2, keepdims=True), jnp.max(group_scores, axis=2, keepdims=True)
    )
    prior_weights = jnp.exp(prior_scores - row_top)
    group_weights = jnp.exp(group_scores - row_top)
    weight_total = jnp.sum(prior_weights, axis=2) + jnp.sum(group_weights, axis=2)
    combined = jnp.einsum(
        "hqk,khd->qhd",
        prior_weights.astype(jnp.bfloat16),
        stored_values,
        preferred_element_type=jnp.float32,
    )
    combined = combined + jnp.einsum(
        "hqk,khd->qhd",
        group_weights.astype(jnp.bfloat16),
        group_values,
        preferred_element_type=jnp.float32,
    )
    prefill_attended = (
        (combined / jnp.transpose(weight_total)[:, :, None])
        .reshape(group_rows, local_width)
        .astype(jnp.bfloat16)
    )

    model_size = out_columns.shape[0] // local_width
    column_start = model_index * local_width

    def send_shares(attended):
        terms = lax.dot_general(
            attended, out_columns, (((1,), (1,)), ((), ())), preferred_element_type=jnp.float32
        ).astype(jnp.bfloat16)
        return jnp.transpose(terms.reshape(terms.shape[0], model_size, local_width), (1, 0, 2))

    def exchange(shares):
        return lax.all_to_all(shares, "fsdp", 0, 0, tiled=False)

    def mixed(received, own_tokens):
        branch = jnp.sum(received.astype(jnp.float32), axis=0)
        residual = lax.dynamic_slice_in_dim(own_tokens, column_start, local_width, 1)
        return (residual.astype(jnp.float32) + branch).astype(jnp.bfloat16)

    prefill_shares, all_decode = lax.optimization_barrier(
        (send_shares(prefill_attended), all_decode)
    )
    prefill_received = exchange(prefill_shares)
    decode_q, decode_k, decode_v = project(all_decode)
    slot_queries = rotary(decode_q, decode_positions, HEAD).astype(jnp.bfloat16)
    slot_keys = rotary(decode_k, decode_positions, HEAD).astype(jnp.bfloat16)
    slot_values = decode_v.astype(jnp.bfloat16)
    own_start = data_index * decode_rows
    own_queries = lax.dynamic_slice_in_dim(slot_queries, own_start, decode_rows, 0)
    own_keys = lax.dynamic_slice_in_dim(slot_keys, own_start, decode_rows, 0)
    own_values = lax.dynamic_slice_in_dim(slot_values, own_start, decode_rows, 0)
    pool_count = page_slots.shape[0]
    pool_local = pool_keys.shape[0]
    local_slots = data_index * pool_local + jnp.arange(pool_local, dtype=jnp.int32)
    slot_hit = page_slots[None, :] == local_slots[:, None]
    local_logical = jnp.sum(
        jnp.where(slot_hit, jnp.arange(pool_count, dtype=jnp.int32)[None, :], 0), axis=1
    )
    page_owner = (
        jnp.sum((first_page[None, :] <= local_logical[:, None]).astype(jnp.int32), axis=1) - 1
    )
    page_number = local_logical - jnp.take(first_page, page_owner)
    page_slot = jnp.take(slot_of_request, page_owner)
    page_queries = jnp.take(slot_queries, page_slot, axis=0).reshape(pool_local, head_count, HEAD)
    page_keys = pool_keys.reshape(pool_local, PAGE, head_count, HEAD)
    page_scores = (
        jnp.einsum("phd,pkhd->phk", page_queries, page_keys, preferred_element_type=jnp.float32)
        * score_scale
    )
    key_place = page_number[:, None] * PAGE + jnp.arange(PAGE, dtype=jnp.int32)[None, :]
    page_live = key_place < jnp.take(cache_length, page_owner)[:, None]
    page_scores = jnp.where(page_live[:, None, :], page_scores, NEG_FILL)
    member = page_slot[:, None] == slot_numbers[None, :]
    page_top = jnp.max(page_scores, axis=2)
    slot_top = jnp.max(jnp.where(member[:, :, None], page_top[:, None, :], NEG_FILL), axis=0)
    page_weights = jnp.exp(page_scores - jnp.take(slot_top, page_slot, axis=0)[:, :, None])
    member_weights = member.astype(jnp.float32)
    slot_total = jnp.dot(
        member_weights.T, jnp.sum(page_weights, axis=2), precision=lax.Precision.HIGHEST
    )
    page_values = pool_values.reshape(pool_local, PAGE, head_count, HEAD).astype(jnp.float32)
    page_mix = jnp.einsum(
        "phk,pkhd->phd", page_weights, page_values, precision=lax.Precision.HIGHEST
    )
    slot_mix = jnp.dot(
        member_weights.T, page_mix.reshape(pool_local, local_width), precision=lax.Precision.HIGHEST
    )
    partials = jnp.concatenate([slot_top, slot_total, slot_mix], axis=1)
    partials, prefill_received = lax.optimization_barrier((partials, prefill_received))
    received = lax.all_to_all(
        partials.reshape(dp_size, decode_rows, -1), "dp", 0, 0, tiled=False
    )
    source_top = received[:, :, :head_count]
    source_total = received[:, :, head_count : 2 * head_count]
    source_mix = received[:, :, 2 * head_count :]
    mine_top = jnp.max(source_top, axis=0)
    source_factor = jnp.exp(source_top - mine_top[None])
    mine_total = jnp.sum(source_total * source_factor, axis=0)
    mine_mix = jnp.sum(
        source_mix.reshape(dp_size, decode_rows, head_count, HEAD) * source_factor[..., None], axis=0
    ).reshape(decode_rows, local_width)
    own_score = (
        jnp.einsum(
            "rhd,rhd->rh",
            own_queries.reshape(decode_rows, head_count, HEAD),
            own_keys.reshape(decode_rows, head_count, HEAD),
            preferred_element_type=jnp.float32,
        )
        * score_scale
    )
    final_top = jnp.maximum(mine_top, own_score)
    cache_factor = jnp.exp(mine_top - final_top)
    own_factor = jnp.exp(own_score - final_top)
    final_total = mine_total * cache_factor + own_factor
    final_mix = rescale(mine_mix, cache_factor, HEAD) + rescale(
        own_values.astype(jnp.float32), own_factor, HEAD
    )
    decode_attended = rescale(final_mix, 1.0 / final_total, HEAD).astype(jnp.bfloat16)
    return (
        mixed(prefill_received, prefill_tokens),
        mixed(exchange(send_shares(decode_attended)), decode_tokens),
    )


def solution(mesh):
    in_specs = (
        P("dp", None),
        P("dp", None),
        P("dp", "fsdp"),
        P("dp", "fsdp"),
        P("dp", "fsdp"),
        P("fsdp", "dp"),
        P("dp", None, "fsdp"),
        P("dp", None, "fsdp"),
        P("dp"),
        P("dp", None, "fsdp"),
        P("dp", None, "fsdp"),
        P(),
        P(),
        P(),
        P(),
    )
    out_specs = (P("dp", "fsdp"), P("dp", "fsdp"))
    return jax.shard_map(
        functools.partial(per_device, dp_size=mesh.shape["dp"]),
        mesh=mesh,
        in_specs=in_specs,
        out_specs=out_specs,
        check_vma=False,
    )
```

```python
import functools

import jax
import jax.numpy as jnp
from jax import lax
from jax.sharding import Mesh, PartitionSpec as P

HEAD = 128
PAGE = 128


EPSILON = 1e-05
ROPE_BASE = 10000.0
NEG_FILL = -1e30
DP = ("dy", "dz")


def layer_norm(rows_in):
    widened = rows_in.astype(jnp.float32)
    average = jnp.mean(widened, axis=-1, keepdims=True)
    centred = widened - average
    variance = jnp.mean(centred * centred, axis=-1, keepdims=True)
    return (centred * lax.rsqrt(variance + EPSILON)).astype(jnp.bfloat16)


def rotary(vectors, positions, head_size):
    row_count = vectors.shape[0]
    split_heads = vectors.reshape(row_count, -1, head_size)
    halfway = head_size // 2
    exponent = jnp.arange(halfway, dtype=jnp.float32) * (2.0 / head_size)
    frequency = jnp.power(jnp.float32(ROPE_BASE), -exponent)
    angles = positions.astype(jnp.float32)[:, None] * frequency[None, :]
    cosine = jnp.cos(angles)[:, None, :]
    sine_part = jnp.sin(angles)[:, None, :]
    leading = split_heads[..., :halfway]
    trailing = split_heads[..., halfway:]
    turned = jnp.concatenate(
        [leading * cosine - trailing * sine_part, trailing * cosine + leading * sine_part], axis=-1
    )
    return turned.reshape(row_count, -1)


def rescale(vectors, factor, head_size):
    shaped = vectors.reshape(vectors.shape[0], factor.shape[1], head_size)
    return (shaped * factor[:, :, None]).reshape(vectors.shape)


def inverse_permutation(order):
    count = order.shape[0]
    numbers = jnp.arange(count, dtype=jnp.int32)
    hit = order[None, :] == numbers[:, None]
    return jnp.sum(jnp.where(hit, numbers[None, :], 0), axis=1)


def per_device(
    prefill_tokens,
    decode_tokens,
    query_weight,
    key_weight,
    value_weight,
    out_weight,
    prior_keys,
    prior_values,
    prior_length,
    pool_keys,
    pool_values,
    page_slots,
    page_counts,
    last_fill,
    decode_request,
    *,
    dp_size,
):
    group_rows = prefill_tokens.shape[0]
    decode_rows = decode_tokens.shape[0]
    weight_rows = query_weight.shape[0]
    local_width = query_weight.shape[1]
    head_count = local_width // HEAD
    score_scale = HEAD ** (-0.5)
    data_index = lax.axis_index(DP)
    model_index = lax.axis_index("fsdp")

    decode_piece = decode_tokens.reshape(-1, local_width)
    decode_piece = jnp.pad(decode_piece, ((0, weight_rows - decode_piece.shape[0]), (0, 0)))
    bundle = jnp.stack(
        [query_weight, key_weight, value_weight, jnp.transpose(out_weight), decode_piece]
    )
    across_y = lax.all_gather(bundle, "dy", axis=1, tiled=False)
    gathered = lax.all_gather(across_y, "dz", axis=2, tiled=False).reshape(
        bundle.shape[0], dp_size * weight_rows, local_width
    )
    projection_weights = [gathered[p] for p in range(3)]
    out_columns = gathered[3]
    decode_size = decode_tokens.size
    all_decode = (
        gathered[4].reshape(dp_size, -1)[:, :decode_size].reshape(dp_size * decode_rows, -1)
    )

    def project(rows_in):
        normed = layer_norm(rows_in)
        return tuple(
            jnp.dot(normed, weight, preferred_element_type=jnp.float32)
            for weight in projection_weights
        )

    cache_length = (page_counts - 1) * PAGE + last_fill
    first_page = jnp.cumsum(page_counts) - page_counts
    request_count = decode_request.shape[0]
    slot_numbers = jnp.arange(request_count, dtype=jnp.int32)
    slot_of_request = inverse_permutation(decode_request)
    prefill_q, prefill_k, prefill_v = project(prefill_tokens)
    prefill_positions = prior_length[0] + jnp.arange(group_rows, dtype=jnp.int32)
    decode_positions = jnp.take(cache_length, decode_request)
    group_queries = rotary(prefill_q, prefill_positions, HEAD).astype(jnp.bfloat16)
    group_keys = rotary(prefill_k, prefill_positions, HEAD).astype(jnp.bfloat16)
    group_values = prefill_v.astype(jnp.bfloat16)

    prior_slots = prior_keys.shape[1]
    group_queries = group_queries.reshape(group_rows, head_count, HEAD)
    group_keys = group_keys.reshape(group_rows, head_count, HEAD)
    group_values = group_values.reshape(group_rows, head_count, HEAD)
    stored_keys = prior_keys[0].reshape(prior_slots, head_count, HEAD)
    stored_values = prior_values[0].reshape(prior_slots, head_count, HEAD)
    prior_scores = (
        jnp.einsum("qhd,khd->hqk", group_queries, stored_keys, preferred_element_type=jnp.float32)
        * score_scale
    )
    prior_live = jnp.arange(prior_slots, dtype=jnp.int32) < prior_length[0]
    prior_scores = jnp.where(prior_live[None, None, :], prior_scores, NEG_FILL)
    group_scores = (
        jnp.einsum("qhd,khd->hqk", group_queries, group_keys, preferred_element_type=jnp.float32)
        * score_scale
    )
    causal = jnp.arange(group_rows)[None, :] <= jnp.arange(group_rows)[:, None]
    group_scores = jnp.where(causal[None], group_scores, NEG_FILL)
    row_top = jnp.maximum(
        jnp.max(prior_scores, axis=2, keepdims=True), jnp.max(group_scores, axis=2, keepdims=True)
    )
    prior_weights = jnp.exp(prior_scores - row_top)
    group_weights = jnp.exp(group_scores - row_top)
    weight_total = jnp.sum(prior_weights, axis=2) + jnp.sum(group_weights, axis=2)
    combined = jnp.einsum(
        "hqk,khd->qhd",
        prior_weights.astype(jnp.bfloat16),
        stored_values,
        preferred_element_type=jnp.float32,
    )
    combined = combined + jnp.einsum(
        "hqk,khd->qhd",
        group_weights.astype(jnp.bfloat16),
        group_values,
        preferred_element_type=jnp.float32,
    )
    prefill_attended = (
        (combined / jnp.transpose(weight_total)[:, :, None])
        .reshape(group_rows, local_width)
        .astype(jnp.bfloat16)
    )

    model_size = out_columns.shape[0] // local_width
    column_start = model_index * local_width

    def send_shares(attended):
        terms = lax.dot_general(
            attended, out_columns, (((1,), (1,)), ((), ())), preferred_element_type=jnp.float32
        ).astype(jnp.bfloat16)
        return jnp.transpose(terms.reshape(terms.shape[0], model_size, local_width), (1, 0, 2))

    def exchange(shares):
        return lax.all_to_all(shares, "fsdp", 0, 0, tiled=False)

    def mixed(received, own_tokens):
        branch = jnp.sum(received.astype(jnp.float32), axis=0)
        residual = lax.dynamic_slice_in_dim(own_tokens, column_start, local_width, 1)
        return (residual.astype(jnp.float32) + branch).astype(jnp.bfloat16)

    prefill_shares, all_decode = lax.optimization_barrier(
        (send_shares(prefill_attended), all_decode)
    )
    prefill_received = exchange(prefill_shares)
    decode_q, decode_k, decode_v = project(all_decode)
    slot_queries = rotary(decode_q, decode_positions, HEAD).astype(jnp.bfloat16)
    slot_keys = rotary(decode_k, decode_positions, HEAD).astype(jnp.bfloat16)
    slot_values = decode_v.astype(jnp.bfloat16)
    own_start = data_index * decode_rows
    own_queries = lax.dynamic_slice_in_dim(slot_queries, own_start, decode_rows, 0)
    own_keys = lax.dynamic_slice_in_dim(slot_keys, own_start, decode_rows, 0)
    own_values = lax.dynamic_slice_in_dim(slot_values, own_start, decode_rows, 0)
    pool_count = page_slots.shape[0]
    pool_local = pool_keys.shape[0]
    local_slots = data_index * pool_local + jnp.arange(pool_local, dtype=jnp.int32)
    slot_hit = page_slots[None, :] == local_slots[:, None]
    local_logical = jnp.sum(
        jnp.where(slot_hit, jnp.arange(pool_count, dtype=jnp.int32)[None, :], 0), axis=1
    )
    page_owner = (
        jnp.sum((first_page[None, :] <= local_logical[:, None]).astype(jnp.int32), axis=1) - 1
    )
    page_number = local_logical - jnp.take(first_page, page_owner)
    page_slot = jnp.take(slot_of_request, page_owner)
    page_queries = jnp.take(slot_queries, page_slot, axis=0).reshape(pool_local, head_count, HEAD)
    page_keys = pool_keys.reshape(pool_local, PAGE, head_count, HEAD)
    page_scores = (
        jnp.einsum("phd,pkhd->phk", page_queries, page_keys, preferred_element_type=jnp.float32)
        * score_scale
    )
    key_place = page_number[:, None] * PAGE + jnp.arange(PAGE, dtype=jnp.int32)[None, :]
    page_live = key_place < jnp.take(cache_length, page_owner)[:, None]
    page_scores = jnp.where(page_live[:, None, :], page_scores, NEG_FILL)
    member = page_slot[:, None] == slot_numbers[None, :]
    page_top = jnp.max(page_scores, axis=2)
    slot_top = jnp.max(jnp.where(member[:, :, None], page_top[:, None, :], NEG_FILL), axis=0)
    page_weights = jnp.exp(page_scores - jnp.take(slot_top, page_slot, axis=0)[:, :, None])
    member_weights = member.astype(jnp.float32)
    slot_total = jnp.dot(
        member_weights.T, jnp.sum(page_weights, axis=2), precision=lax.Precision.HIGHEST
    )
    page_values = pool_values.reshape(pool_local, PAGE, head_count, HEAD).astype(jnp.float32)
    page_mix = jnp.einsum(
        "phk,pkhd->phd", page_weights, page_values, precision=lax.Precision.HIGHEST
    )
    slot_mix = jnp.dot(
        member_weights.T, page_mix.reshape(pool_local, local_width), precision=lax.Precision.HIGHEST
    )
    partials = jnp.concatenate([slot_top, slot_total, slot_mix], axis=1)
    partials, prefill_received = lax.optimization_barrier((partials, prefill_received))
    received = lax.all_to_all(
        partials.reshape(dp_size, decode_rows, -1), DP, 0, 0, tiled=False
    )
    source_top = received[:, :, :head_count]
    source_total = received[:, :, head_count : 2 * head_count]
    source_mix = received[:, :, 2 * head_count :]
    mine_top = jnp.max(source_top, axis=0)
    source_factor = jnp.exp(source_top - mine_top[None])
    mine_total = jnp.sum(source_total * source_factor, axis=0)
    mine_mix = jnp.sum(
        source_mix.reshape(dp_size, decode_rows, head_count, HEAD) * source_factor[..., None], axis=0
    ).reshape(decode_rows, local_width)
    own_score = (
        jnp.einsum(
            "rhd,rhd->rh",
            own_queries.reshape(decode_rows, head_count, HEAD),
            own_keys.reshape(decode_rows, head_count, HEAD),
            preferred_element_type=jnp.float32,
        )
        * score_scale
    )
    final_top = jnp.maximum(mine_top, own_score)
    cache_factor = jnp.exp(mine_top - final_top)
    own_factor = jnp.exp(own_score - final_top)
    final_total = mine_total * cache_factor + own_factor
    final_mix = rescale(mine_mix, cache_factor, HEAD) + rescale(
        own_values.astype(jnp.float32), own_factor, HEAD
    )
    decode_attended = rescale(final_mix, 1.0 / final_total, HEAD).astype(jnp.bfloat16)
    return (
        mixed(prefill_received, prefill_tokens),
        mixed(exchange(send_shares(decode_attended)), decode_tokens),
    )


def solution(mesh):
    dp_size = mesh.shape["dp"]
    split_mesh = Mesh(
        mesh.devices.reshape(4, dp_size // 4, mesh.shape["fsdp"]), ("dy", "dz", "fsdp")
    )
    in_specs = (
        P(DP, None),
        P(DP, None),
        P(DP, "fsdp"),
        P(DP, "fsdp"),
        P(DP, "fsdp"),
        P("fsdp", DP),
        P(DP, None, "fsdp"),
        P(DP, None, "fsdp"),
        P(DP),
        P(DP, None, "fsdp"),
        P(DP, None, "fsdp"),
        P(),
        P(),
        P(),
        P(),
    )
    out_specs = (P(DP, "fsdp"), P(DP, "fsdp"))
    return jax.shard_map(
        functools.partial(per_device, dp_size=dp_size),
        mesh=split_mesh,
        in_specs=in_specs,
        out_specs=out_specs,
        check_vma=False,
    )
```

```python
import functools

import jax
import jax.numpy as jnp
from jax import lax
from jax.sharding import Mesh, PartitionSpec as P

HEAD = 128
PAGE = 128


EPSILON = 1e-05
ROPE_BASE = 10000.0
NEG_FILL = -1e30
DP = ("dy", "dz")


def layer_norm(rows_in):
    widened = rows_in.astype(jnp.float32)
    average = jnp.mean(widened, axis=-1, keepdims=True)
    centred = widened - average
    variance = jnp.mean(centred * centred, axis=-1, keepdims=True)
    return (centred * lax.rsqrt(variance + EPSILON)).astype(jnp.bfloat16)


def rotary(vectors, positions, head_size):
    row_count = vectors.shape[0]
    split_heads = vectors.reshape(row_count, -1, head_size)
    halfway = head_size // 2
    exponent = jnp.arange(halfway, dtype=jnp.float32) * (2.0 / head_size)
    frequency = jnp.power(jnp.float32(ROPE_BASE), -exponent)
    angles = positions.astype(jnp.float32)[:, None] * frequency[None, :]
    cosine = jnp.cos(angles)[:, None, :]
    sine_part = jnp.sin(angles)[:, None, :]
    leading = split_heads[..., :halfway]
    trailing = split_heads[..., halfway:]
    turned = jnp.concatenate(
        [leading * cosine - trailing * sine_part, trailing * cosine + leading * sine_part], axis=-1
    )
    return turned.reshape(row_count, -1)


def rescale(vectors, factor, head_size):
    shaped = vectors.reshape(vectors.shape[0], factor.shape[1], head_size)
    return (shaped * factor[:, :, None]).reshape(vectors.shape)


def inverse_permutation(order):
    count = order.shape[0]
    numbers = jnp.arange(count, dtype=jnp.int32)
    hit = order[None, :] == numbers[:, None]
    return jnp.sum(jnp.where(hit, numbers[None, :], 0), axis=1)


def per_device(
    prefill_tokens,
    decode_tokens,
    query_weight,
    key_weight,
    value_weight,
    out_weight,
    prior_keys,
    prior_values,
    prior_length,
    pool_keys,
    pool_values,
    page_slots,
    page_counts,
    last_fill,
    decode_request,
    *,
    dp_size,
):
    group_rows = prefill_tokens.shape[0]
    decode_rows = decode_tokens.shape[0]
    weight_rows = query_weight.shape[0]
    local_width = query_weight.shape[1]
    head_count = local_width // HEAD
    score_scale = HEAD ** (-0.5)
    data_index = lax.axis_index(DP)
    model_index = lax.axis_index("fsdp")

    decode_piece = decode_tokens.reshape(-1, local_width)
    decode_piece = jnp.pad(decode_piece, ((0, weight_rows - decode_piece.shape[0]), (0, 0)))
    bundle = jnp.stack(
        [query_weight, key_weight, value_weight, jnp.transpose(out_weight), decode_piece]
    )
    across_y = lax.all_gather(bundle, "dy", axis=1, tiled=False)
    gathered = lax.all_gather(across_y, "dz", axis=2, tiled=False).reshape(
        bundle.shape[0], dp_size * weight_rows, local_width
    )
    projection_weights = [gathered[p] for p in range(3)]
    out_columns = gathered[3]
    decode_size = decode_tokens.size
    all_decode = (
        gathered[4].reshape(dp_size, -1)[:, :decode_size].reshape(dp_size * decode_rows, -1)
    )

    def project(rows_in):
        normed = layer_norm(rows_in)
        return tuple(
            jnp.dot(normed, weight, preferred_element_type=jnp.float32)
            for weight in projection_weights
        )

    cache_length = (page_counts - 1) * PAGE + last_fill
    first_page = jnp.cumsum(page_counts) - page_counts
    request_count = decode_request.shape[0]
    slot_numbers = jnp.arange(request_count, dtype=jnp.int32)
    slot_of_request = inverse_permutation(decode_request)
    prefill_q, prefill_k, prefill_v = project(prefill_tokens)
    prefill_positions = prior_length[0] + jnp.arange(group_rows, dtype=jnp.int32)
    decode_positions = jnp.take(cache_length, decode_request)
    group_queries = rotary(prefill_q, prefill_positions, HEAD).astype(jnp.bfloat16)
    group_keys = rotary(prefill_k, prefill_positions, HEAD).astype(jnp.bfloat16)
    group_values = prefill_v.astype(jnp.bfloat16)

    model_size = out_columns.shape[0] // local_width
    column_start = model_index * local_width

    def send_shares(attended):
        terms = lax.dot_general(
            attended, out_columns, (((1,), (1,)), ((), ())), preferred_element_type=jnp.float32
        ).astype(jnp.bfloat16)
        return jnp.transpose(terms.reshape(terms.shape[0], model_size, local_width), (1, 0, 2))

    def exchange(shares):
        return lax.all_to_all(shares, "fsdp", 0, 0, tiled=False)

    def mixed(received, own_tokens):
        branch = jnp.sum(received.astype(jnp.float32), axis=0)
        residual = lax.dynamic_slice_in_dim(own_tokens, column_start, local_width, 1)
        return (residual.astype(jnp.float32) + branch).astype(jnp.bfloat16)

    decode_q, decode_k, decode_v = project(all_decode)
    slot_queries = rotary(decode_q, decode_positions, HEAD).astype(jnp.bfloat16)
    slot_keys = rotary(decode_k, decode_positions, HEAD).astype(jnp.bfloat16)
    slot_values = decode_v.astype(jnp.bfloat16)
    own_start = data_index * decode_rows
    own_queries = lax.dynamic_slice_in_dim(slot_queries, own_start, decode_rows, 0)
    own_keys = lax.dynamic_slice_in_dim(slot_keys, own_start, decode_rows, 0)
    own_values = lax.dynamic_slice_in_dim(slot_values, own_start, decode_rows, 0)
    pool_count = page_slots.shape[0]
    pool_local = pool_keys.shape[0]
    local_slots = data_index * pool_local + jnp.arange(pool_local, dtype=jnp.int32)
    slot_hit = page_slots[None, :] == local_slots[:, None]
    local_logical = jnp.sum(
        jnp.where(slot_hit, jnp.arange(pool_count, dtype=jnp.int32)[None, :], 0), axis=1
    )
    page_owner = (
        jnp.sum((first_page[None, :] <= local_logical[:, None]).astype(jnp.int32), axis=1) - 1
    )
    page_number = local_logical - jnp.take(first_page, page_owner)
    page_slot = jnp.take(slot_of_request, page_owner)
    page_queries = jnp.take(slot_queries, page_slot, axis=0).reshape(pool_local, head_count, HEAD)
    page_keys = pool_keys.reshape(pool_local, PAGE, head_count, HEAD)
    page_scores = (
        jnp.einsum("phd,pkhd->phk", page_queries, page_keys, preferred_element_type=jnp.float32)
        * score_scale
    )
    key_place = page_number[:, None] * PAGE + jnp.arange(PAGE, dtype=jnp.int32)[None, :]
    page_live = key_place < jnp.take(cache_length, page_owner)[:, None]
    page_scores = jnp.where(page_live[:, None, :], page_scores, NEG_FILL)
    member = page_slot[:, None] == slot_numbers[None, :]
    page_top = jnp.max(page_scores, axis=2)
    slot_top = jnp.max(jnp.where(member[:, :, None], page_top[:, None, :], NEG_FILL), axis=0)
    page_weights = jnp.exp(page_scores - jnp.take(slot_top, page_slot, axis=0)[:, :, None])
    member_weights = member.astype(jnp.float32)
    slot_total = jnp.dot(
        member_weights.T, jnp.sum(page_weights, axis=2), precision=lax.Precision.HIGHEST
    )
    page_values = pool_values.reshape(pool_local, PAGE, head_count, HEAD).astype(jnp.float32)
    page_mix = jnp.einsum(
        "phk,pkhd->phd", page_weights, page_values, precision=lax.Precision.HIGHEST
    )
    slot_mix = jnp.dot(
        member_weights.T, page_mix.reshape(pool_local, local_width), precision=lax.Precision.HIGHEST
    )
    partials = jnp.concatenate([slot_top, slot_total, slot_mix], axis=1)
    partials, group_queries, group_keys, group_values = lax.optimization_barrier(
        (partials, group_queries, group_keys, group_values)
    )
    prior_slots = prior_keys.shape[1]
    group_queries = group_queries.reshape(group_rows, head_count, HEAD)
    group_keys = group_keys.reshape(group_rows, head_count, HEAD)
    group_values = group_values.reshape(group_rows, head_count, HEAD)
    stored_keys = prior_keys[0].reshape(prior_slots, head_count, HEAD)
    stored_values = prior_values[0].reshape(prior_slots, head_count, HEAD)
    prior_scores = (
        jnp.einsum("qhd,khd->hqk", group_queries, stored_keys, preferred_element_type=jnp.float32)
        * score_scale
    )
    prior_live = jnp.arange(prior_slots, dtype=jnp.int32) < prior_length[0]
    prior_scores = jnp.where(prior_live[None, None, :], prior_scores, NEG_FILL)
    group_scores = (
        jnp.einsum("qhd,khd->hqk", group_queries, group_keys, preferred_element_type=jnp.float32)
        * score_scale
    )
    causal = jnp.arange(group_rows)[None, :] <= jnp.arange(group_rows)[:, None]
    group_scores = jnp.where(causal[None], group_scores, NEG_FILL)
    row_top = jnp.maximum(
        jnp.max(prior_scores, axis=2, keepdims=True), jnp.max(group_scores, axis=2, keepdims=True)
    )
    prior_weights = jnp.exp(prior_scores - row_top)
    group_weights = jnp.exp(group_scores - row_top)
    weight_total = jnp.sum(prior_weights, axis=2) + jnp.sum(group_weights, axis=2)
    combined = jnp.einsum(
        "hqk,khd->qhd",
        prior_weights.astype(jnp.bfloat16),
        stored_values,
        preferred_element_type=jnp.float32,
    )
    combined = combined + jnp.einsum(
        "hqk,khd->qhd",
        group_weights.astype(jnp.bfloat16),
        group_values,
        preferred_element_type=jnp.float32,
    )
    prefill_attended = (
        (combined / jnp.transpose(weight_total)[:, :, None])
        .reshape(group_rows, local_width)
        .astype(jnp.bfloat16)
    )

    received = lax.all_to_all(
        partials.reshape(dp_size, decode_rows, -1), DP, 0, 0, tiled=False
    )
    source_top = received[:, :, :head_count]
    source_total = received[:, :, head_count : 2 * head_count]
    source_mix = received[:, :, 2 * head_count :]
    mine_top = jnp.max(source_top, axis=0)
    source_factor = jnp.exp(source_top - mine_top[None])
    mine_total = jnp.sum(source_total * source_factor, axis=0)
    mine_mix = jnp.sum(
        source_mix.reshape(dp_size, decode_rows, head_count, HEAD) * source_factor[..., None], axis=0
    ).reshape(decode_rows, local_width)
    own_score = (
        jnp.einsum(
            "rhd,rhd->rh",
            own_queries.reshape(decode_rows, head_count, HEAD),
            own_keys.reshape(decode_rows, head_count, HEAD),
            preferred_element_type=jnp.float32,
        )
        * score_scale
    )
    final_top = jnp.maximum(mine_top, own_score)
    cache_factor = jnp.exp(mine_top - final_top)
    own_factor = jnp.exp(own_score - final_top)
    final_total = mine_total * cache_factor + own_factor
    final_mix = rescale(mine_mix, cache_factor, HEAD) + rescale(
        own_values.astype(jnp.float32), own_factor, HEAD
    )
    decode_attended = rescale(final_mix, 1.0 / final_total, HEAD).astype(jnp.bfloat16)
    attended = jnp.concatenate([prefill_attended, decode_attended], axis=0)
    own_tokens = jnp.concatenate([prefill_tokens, decode_tokens], axis=0)
    result = mixed(exchange(send_shares(attended)), own_tokens)
    return (result[:group_rows], result[group_rows:])


def solution(mesh):
    dp_size = mesh.shape["dp"]
    split_mesh = Mesh(
        mesh.devices.reshape(4, dp_size // 4, mesh.shape["fsdp"]), ("dy", "dz", "fsdp")
    )
    in_specs = (
        P(DP, None),
        P(DP, None),
        P(DP, "fsdp"),
        P(DP, "fsdp"),
        P(DP, "fsdp"),
        P("fsdp", DP),
        P(DP, None, "fsdp"),
        P(DP, None, "fsdp"),
        P(DP),
        P(DP, None, "fsdp"),
        P(DP, None, "fsdp"),
        P(),
        P(),
        P(),
        P(),
    )
    out_specs = (P(DP, "fsdp"), P(DP, "fsdp"))
    return jax.shard_map(
        functools.partial(per_device, dp_size=dp_size),
        mesh=split_mesh,
        in_specs=in_specs,
        out_specs=out_specs,
        check_vma=False,
    )
```

```python
import functools

import jax
import jax.numpy as jnp
from jax import lax
from jax.sharding import Mesh, PartitionSpec as P

HEAD = 128
PAGE = 128


EPSILON = 1e-05
ROPE_BASE = 10000.0
NEG_FILL = -1e30
DP = ("dy", "dz")


def layer_norm(rows_in):
    widened = rows_in.astype(jnp.float32)
    average = jnp.mean(widened, axis=-1, keepdims=True)
    centred = widened - average
    variance = jnp.mean(centred * centred, axis=-1, keepdims=True)
    return (centred * lax.rsqrt(variance + EPSILON)).astype(jnp.bfloat16)


def rotary(vectors, positions, head_size):
    row_count = vectors.shape[0]
    split_heads = vectors.reshape(row_count, -1, head_size)
    halfway = head_size // 2
    exponent = jnp.arange(halfway, dtype=jnp.float32) * (2.0 / head_size)
    frequency = jnp.power(jnp.float32(ROPE_BASE), -exponent)
    angles = positions.astype(jnp.float32)[:, None] * frequency[None, :]
    cosine = jnp.cos(angles)[:, None, :]
    sine_part = jnp.sin(angles)[:, None, :]
    leading = split_heads[..., :halfway]
    trailing = split_heads[..., halfway:]
    turned = jnp.concatenate(
        [leading * cosine - trailing * sine_part, trailing * cosine + leading * sine_part], axis=-1
    )
    return turned.reshape(row_count, -1)


def rescale(vectors, factor, head_size):
    shaped = vectors.reshape(vectors.shape[0], factor.shape[1], head_size)
    return (shaped * factor[:, :, None]).reshape(vectors.shape)


def inverse_permutation(order):
    count = order.shape[0]
    numbers = jnp.arange(count, dtype=jnp.int32)
    hit = order[None, :] == numbers[:, None]
    return jnp.sum(jnp.where(hit, numbers[None, :], 0), axis=1)


def per_device(
    prefill_tokens,
    decode_tokens,
    query_weight,
    key_weight,
    value_weight,
    out_weight,
    prior_keys,
    prior_values,
    prior_length,
    pool_keys,
    pool_values,
    page_slots,
    page_counts,
    last_fill,
    decode_request,
    *,
    dp_size,
):
    group_rows = prefill_tokens.shape[0]
    decode_rows = decode_tokens.shape[0]
    weight_rows = query_weight.shape[0]
    local_width = query_weight.shape[1]
    head_count = local_width // HEAD
    score_scale = HEAD ** (-0.5)
    data_index = lax.axis_index(DP)
    model_index = lax.axis_index("fsdp")

    decode_piece = decode_tokens.reshape(-1, local_width)
    decode_piece = jnp.pad(decode_piece, ((0, weight_rows - decode_piece.shape[0]), (0, 0)))
    bundle = jnp.stack(
        [query_weight, key_weight, value_weight, jnp.transpose(out_weight), decode_piece]
    )
    across_y = lax.all_gather(bundle, "dy", axis=1, tiled=False)
    gathered = lax.all_gather(across_y, "dz", axis=2, tiled=False).reshape(
        bundle.shape[0], dp_size * weight_rows, local_width
    )
    projection_weights = [gathered[p] for p in range(3)]
    out_columns = gathered[3]
    decode_size = decode_tokens.size
    all_decode = (
        gathered[4].reshape(dp_size, -1)[:, :decode_size].reshape(dp_size * decode_rows, -1)
    )

    def project(rows_in):
        normed = layer_norm(rows_in)
        return tuple(
            jnp.dot(normed, weight, preferred_element_type=jnp.float32)
            for weight in projection_weights
        )

    cache_length = (page_counts - 1) * PAGE + last_fill
    first_page = jnp.cumsum(page_counts) - page_counts
    request_count = decode_request.shape[0]
    slot_numbers = jnp.arange(request_count, dtype=jnp.int32)
    slot_of_request = inverse_permutation(decode_request)
    prefill_q, prefill_k, prefill_v = project(prefill_tokens)
    prefill_positions = prior_length[0] + jnp.arange(group_rows, dtype=jnp.int32)
    decode_positions = jnp.take(cache_length, decode_request)
    group_queries = rotary(prefill_q, prefill_positions, HEAD).astype(jnp.bfloat16)
    group_keys = rotary(prefill_k, prefill_positions, HEAD).astype(jnp.bfloat16)
    group_values = prefill_v.astype(jnp.bfloat16)

    decode_q, decode_k, decode_v = project(all_decode)
    slot_queries = rotary(decode_q, decode_positions, HEAD).astype(jnp.bfloat16)
    slot_keys = rotary(decode_k, decode_positions, HEAD).astype(jnp.bfloat16)
    slot_values = decode_v.astype(jnp.bfloat16)
    group_queries, group_keys, group_values, slot_queries = lax.optimization_barrier(
        (group_queries, group_keys, group_values, slot_queries)
    )
    prior_slots = prior_keys.shape[1]
    group_queries = group_queries.reshape(group_rows, head_count, HEAD)
    group_keys = group_keys.reshape(group_rows, head_count, HEAD)
    group_values = group_values.reshape(group_rows, head_count, HEAD)
    stored_keys = prior_keys[0].reshape(prior_slots, head_count, HEAD)
    stored_values = prior_values[0].reshape(prior_slots, head_count, HEAD)
    prior_scores = (
        jnp.einsum("qhd,khd->hqk", group_queries, stored_keys, preferred_element_type=jnp.float32)
        * score_scale
    )
    prior_live = jnp.arange(prior_slots, dtype=jnp.int32) < prior_length[0]
    prior_scores = jnp.where(prior_live[None, None, :], prior_scores, NEG_FILL)
    group_scores = (
        jnp.einsum("qhd,khd->hqk", group_queries, group_keys, preferred_element_type=jnp.float32)
        * score_scale
    )
    causal = jnp.arange(group_rows)[None, :] <= jnp.arange(group_rows)[:, None]
    group_scores = jnp.where(causal[None], group_scores, NEG_FILL)
    row_top = jnp.maximum(
        jnp.max(prior_scores, axis=2, keepdims=True), jnp.max(group_scores, axis=2, keepdims=True)
    )
    prior_weights = jnp.exp(prior_scores - row_top)
    group_weights = jnp.exp(group_scores - row_top)
    weight_total = jnp.sum(prior_weights, axis=2) + jnp.sum(group_weights, axis=2)
    combined = jnp.einsum(
        "hqk,khd->qhd",
        prior_weights.astype(jnp.bfloat16),
        stored_values,
        preferred_element_type=jnp.float32,
    )
    combined = combined + jnp.einsum(
        "hqk,khd->qhd",
        group_weights.astype(jnp.bfloat16),
        group_values,
        preferred_element_type=jnp.float32,
    )
    prefill_attended = (
        (combined / jnp.transpose(weight_total)[:, :, None])
        .reshape(group_rows, local_width)
        .astype(jnp.bfloat16)
    )

    model_size = out_columns.shape[0] // local_width
    column_start = model_index * local_width

    def send_shares(attended):
        terms = lax.dot_general(
            attended, out_columns, (((1,), (1,)), ((), ())), preferred_element_type=jnp.float32
        ).astype(jnp.bfloat16)
        return jnp.transpose(terms.reshape(terms.shape[0], model_size, local_width), (1, 0, 2))

    def exchange(shares):
        return lax.all_to_all(shares, "fsdp", 0, 0, tiled=False)

    def mixed(received, own_tokens):
        branch = jnp.sum(received.astype(jnp.float32), axis=0)
        residual = lax.dynamic_slice_in_dim(own_tokens, column_start, local_width, 1)
        return (residual.astype(jnp.float32) + branch).astype(jnp.bfloat16)

    prefill_shares, slot_queries = lax.optimization_barrier(
        (send_shares(prefill_attended), slot_queries)
    )
    prefill_received = exchange(prefill_shares)
    own_start = data_index * decode_rows
    own_queries = lax.dynamic_slice_in_dim(slot_queries, own_start, decode_rows, 0)
    own_keys = lax.dynamic_slice_in_dim(slot_keys, own_start, decode_rows, 0)
    own_values = lax.dynamic_slice_in_dim(slot_values, own_start, decode_rows, 0)
    pool_count = page_slots.shape[0]
    pool_local = pool_keys.shape[0]
    local_slots = data_index * pool_local + jnp.arange(pool_local, dtype=jnp.int32)
    slot_hit = page_slots[None, :] == local_slots[:, None]
    local_logical = jnp.sum(
        jnp.where(slot_hit, jnp.arange(pool_count, dtype=jnp.int32)[None, :], 0), axis=1
    )
    page_owner = (
        jnp.sum((first_page[None, :] <= local_logical[:, None]).astype(jnp.int32), axis=1) - 1
    )
    page_number = local_logical - jnp.take(first_page, page_owner)
    page_slot = jnp.take(slot_of_request, page_owner)
    page_queries = jnp.take(slot_queries, page_slot, axis=0).reshape(pool_local, head_count, HEAD)
    page_keys = pool_keys.reshape(pool_local, PAGE, head_count, HEAD)
    page_scores = (
        jnp.einsum("phd,pkhd->phk", page_queries, page_keys, preferred_element_type=jnp.float32)
        * score_scale
    )
    key_place = page_number[:, None] * PAGE + jnp.arange(PAGE, dtype=jnp.int32)[None, :]
    page_live = key_place < jnp.take(cache_length, page_owner)[:, None]
    page_scores = jnp.where(page_live[:, None, :], page_scores, NEG_FILL)
    member = page_slot[:, None] == slot_numbers[None, :]
    page_top = jnp.max(page_scores, axis=2)
    slot_top = jnp.max(jnp.where(member[:, :, None], page_top[:, None, :], NEG_FILL), axis=0)
    page_weights = jnp.exp(page_scores - jnp.take(slot_top, page_slot, axis=0)[:, :, None])
    member_weights = member.astype(jnp.float32)
    slot_total = jnp.dot(
        member_weights.T, jnp.sum(page_weights, axis=2), precision=lax.Precision.HIGHEST
    )
    page_values = pool_values.reshape(pool_local, PAGE, head_count, HEAD).astype(jnp.float32)
    page_mix = jnp.einsum(
        "phk,pkhd->phd", page_weights, page_values, precision=lax.Precision.HIGHEST
    )
    slot_mix = jnp.dot(
        member_weights.T, page_mix.reshape(pool_local, local_width), precision=lax.Precision.HIGHEST
    )
    partials = jnp.concatenate([slot_top, slot_total, slot_mix], axis=1)
    partials, prefill_received = lax.optimization_barrier((partials, prefill_received))
    received = lax.all_to_all(
        partials.reshape(dp_size, decode_rows, -1), DP, 0, 0, tiled=False
    )
    source_top = received[:, :, :head_count]
    source_total = received[:, :, head_count : 2 * head_count]
    source_mix = received[:, :, 2 * head_count :]
    mine_top = jnp.max(source_top, axis=0)
    source_factor = jnp.exp(source_top - mine_top[None])
    mine_total = jnp.sum(source_total * source_factor, axis=0)
    mine_mix = jnp.sum(
        source_mix.reshape(dp_size, decode_rows, head_count, HEAD) * source_factor[..., None], axis=0
    ).reshape(decode_rows, local_width)
    own_score = (
        jnp.einsum(
            "rhd,rhd->rh",
            own_queries.reshape(decode_rows, head_count, HEAD),
            own_keys.reshape(decode_rows, head_count, HEAD),
            preferred_element_type=jnp.float32,
        )
        * score_scale
    )
    final_top = jnp.maximum(mine_top, own_score)
    cache_factor = jnp.exp(mine_top - final_top)
    own_factor = jnp.exp(own_score - final_top)
    final_total = mine_total * cache_factor + own_factor
    final_mix = rescale(mine_mix, cache_factor, HEAD) + rescale(
        own_values.astype(jnp.float32), own_factor, HEAD
    )
    decode_attended = rescale(final_mix, 1.0 / final_total, HEAD).astype(jnp.bfloat16)
    return (
        mixed(prefill_received, prefill_tokens),
        mixed(exchange(send_shares(decode_attended)), decode_tokens),
    )


def solution(mesh):
    dp_size = mesh.shape["dp"]
    split_mesh = Mesh(
        mesh.devices.reshape(4, dp_size // 4, mesh.shape["fsdp"]), ("dy", "dz", "fsdp")
    )
    in_specs = (
        P(DP, None),
        P(DP, None),
        P(DP, "fsdp"),
        P(DP, "fsdp"),
        P(DP, "fsdp"),
        P("fsdp", DP),
        P(DP, None, "fsdp"),
        P(DP, None, "fsdp"),
        P(DP),
        P(DP, None, "fsdp"),
        P(DP, None, "fsdp"),
        P(),
        P(),
        P(),
        P(),
    )
    out_specs = (P(DP, "fsdp"), P(DP, "fsdp"))
    return jax.shard_map(
        functools.partial(per_device, dp_size=dp_size),
        mesh=split_mesh,
        in_specs=in_specs,
        out_specs=out_specs,
        check_vma=False,
    )
```

```python
import functools

import jax
import jax.numpy as jnp
from jax import lax
from jax.sharding import Mesh, PartitionSpec as P

HEAD = 128
PAGE = 128


EPSILON = 1e-05
ROPE_BASE = 10000.0
NEG_FILL = -1e30
DP = ("dy", "dz")


def layer_norm(rows_in):
    widened = rows_in.astype(jnp.float32)
    average = jnp.mean(widened, axis=-1, keepdims=True)
    centred = widened - average
    variance = jnp.mean(centred * centred, axis=-1, keepdims=True)
    return (centred * lax.rsqrt(variance + EPSILON)).astype(jnp.bfloat16)


def rotary(vectors, positions, head_size):
    row_count = vectors.shape[0]
    split_heads = vectors.reshape(row_count, -1, head_size)
    halfway = head_size // 2
    exponent = jnp.arange(halfway, dtype=jnp.float32) * (2.0 / head_size)
    frequency = jnp.power(jnp.float32(ROPE_BASE), -exponent)
    angles = positions.astype(jnp.float32)[:, None] * frequency[None, :]
    cosine = jnp.cos(angles)[:, None, :]
    sine_part = jnp.sin(angles)[:, None, :]
    leading = split_heads[..., :halfway]
    trailing = split_heads[..., halfway:]
    turned = jnp.concatenate(
        [leading * cosine - trailing * sine_part, trailing * cosine + leading * sine_part], axis=-1
    )
    return turned.reshape(row_count, -1)


def rescale(vectors, factor, head_size):
    shaped = vectors.reshape(vectors.shape[0], factor.shape[1], head_size)
    return (shaped * factor[:, :, None]).reshape(vectors.shape)


def inverse_permutation(order):
    count = order.shape[0]
    numbers = jnp.arange(count, dtype=jnp.int32)
    hit = order[None, :] == numbers[:, None]
    return jnp.sum(jnp.where(hit, numbers[None, :], 0), axis=1)


def per_device(
    prefill_tokens,
    decode_tokens,
    query_weight,
    key_weight,
    value_weight,
    out_weight,
    prior_keys,
    prior_values,
    prior_length,
    pool_keys,
    pool_values,
    page_slots,
    page_counts,
    last_fill,
    decode_request,
    *,
    dp_size,
):
    group_rows = prefill_tokens.shape[0]
    decode_rows = decode_tokens.shape[0]
    weight_rows = query_weight.shape[0]
    local_width = query_weight.shape[1]
    head_count = local_width // HEAD
    score_scale = HEAD ** (-0.5)
    data_index = lax.axis_index(DP)
    model_index = lax.axis_index("fsdp")

    bundle = jnp.stack([query_weight, key_weight, value_weight, jnp.transpose(out_weight)])
    across_y = lax.all_gather(bundle, "dy", axis=1, tiled=False)
    gathered = lax.all_gather(across_y, "dz", axis=2, tiled=False).reshape(
        bundle.shape[0], dp_size * weight_rows, local_width
    )
    projection_weights = [gathered[p] for p in range(3)]
    out_columns = gathered[3]
    all_decode = lax.all_gather(decode_tokens, DP, axis=0, tiled=True)

    def project(rows_in):
        normed = layer_norm(rows_in)
        return tuple(
            jnp.dot(normed, weight, preferred_element_type=jnp.float32)
            for weight in projection_weights
        )

    cache_length = (page_counts - 1) * PAGE + last_fill
    first_page = jnp.cumsum(page_counts) - page_counts
    request_count = decode_request.shape[0]
    slot_numbers = jnp.arange(request_count, dtype=jnp.int32)
    slot_of_request = inverse_permutation(decode_request)
    prefill_q, prefill_k, prefill_v = project(prefill_tokens)
    prefill_positions = prior_length[0] + jnp.arange(group_rows, dtype=jnp.int32)
    decode_positions = jnp.take(cache_length, decode_request)
    group_queries = rotary(prefill_q, prefill_positions, HEAD).astype(jnp.bfloat16)
    group_keys = rotary(prefill_k, prefill_positions, HEAD).astype(jnp.bfloat16)
    group_values = prefill_v.astype(jnp.bfloat16)

    prior_slots = prior_keys.shape[1]
    group_queries = group_queries.reshape(group_rows, head_count, HEAD)
    group_keys = group_keys.reshape(group_rows, head_count, HEAD)
    group_values = group_values.reshape(group_rows, head_count, HEAD)
    stored_keys = prior_keys[0].reshape(prior_slots, head_count, HEAD)
    stored_values = prior_values[0].reshape(prior_slots, head_count, HEAD)
    prior_scores = (
        jnp.einsum("qhd,khd->hqk", group_queries, stored_keys, preferred_element_type=jnp.float32)
        * score_scale
    )
    prior_live = jnp.arange(prior_slots, dtype=jnp.int32) < prior_length[0]
    prior_scores = jnp.where(prior_live[None, None, :], prior_scores, NEG_FILL)
    group_scores = (
        jnp.einsum("qhd,khd->hqk", group_queries, group_keys, preferred_element_type=jnp.float32)
        * score_scale
    )
    causal = jnp.arange(group_rows)[None, :] <= jnp.arange(group_rows)[:, None]
    group_scores = jnp.where(causal[None], group_scores, NEG_FILL)
    row_top = jnp.maximum(
        jnp.max(prior_scores, axis=2, keepdims=True), jnp.max(group_scores, axis=2, keepdims=True)
    )
    prior_weights = jnp.exp(prior_scores - row_top)
    group_weights = jnp.exp(group_scores - row_top)
    weight_total = jnp.sum(prior_weights, axis=2) + jnp.sum(group_weights, axis=2)
    combined = jnp.einsum(
        "hqk,khd->qhd",
        prior_weights.astype(jnp.bfloat16),
        stored_values,
        preferred_element_type=jnp.float32,
    )
    combined = combined + jnp.einsum(
        "hqk,khd->qhd",
        group_weights.astype(jnp.bfloat16),
        group_values,
        preferred_element_type=jnp.float32,
    )
    prefill_attended = (
        (combined / jnp.transpose(weight_total)[:, :, None])
        .reshape(group_rows, local_width)
        .astype(jnp.bfloat16)
    )

    model_size = out_columns.shape[0] // local_width
    column_start = model_index * local_width

    def send_shares(attended):
        terms = lax.dot_general(
            attended, out_columns, (((1,), (1,)), ((), ())), preferred_element_type=jnp.float32
        ).astype(jnp.bfloat16)
        return jnp.transpose(terms.reshape(terms.shape[0], model_size, local_width), (1, 0, 2))

    def exchange(shares):
        return lax.all_to_all(shares, "fsdp", 0, 0, tiled=False)

    def mixed(received, own_tokens):
        branch = jnp.sum(received.astype(jnp.float32), axis=0)
        residual = lax.dynamic_slice_in_dim(own_tokens, column_start, local_width, 1)
        return (residual.astype(jnp.float32) + branch).astype(jnp.bfloat16)

    prefill_shares, all_decode = lax.optimization_barrier(
        (send_shares(prefill_attended), all_decode)
    )
    prefill_received = exchange(prefill_shares)
    decode_q, decode_k, decode_v = project(all_decode)
    slot_queries = rotary(decode_q, decode_positions, HEAD).astype(jnp.bfloat16)
    slot_keys = rotary(decode_k, decode_positions, HEAD).astype(jnp.bfloat16)
    slot_values = decode_v.astype(jnp.bfloat16)
    own_start = data_index * decode_rows
    own_queries = lax.dynamic_slice_in_dim(slot_queries, own_start, decode_rows, 0)
    own_keys = lax.dynamic_slice_in_dim(slot_keys, own_start, decode_rows, 0)
    own_values = lax.dynamic_slice_in_dim(slot_values, own_start, decode_rows, 0)
    pool_count = page_slots.shape[0]
    pool_local = pool_keys.shape[0]
    local_slots = data_index * pool_local + jnp.arange(pool_local, dtype=jnp.int32)
    slot_hit = page_slots[None, :] == local_slots[:, None]
    local_logical = jnp.sum(
        jnp.where(slot_hit, jnp.arange(pool_count, dtype=jnp.int32)[None, :], 0), axis=1
    )
    page_owner = (
        jnp.sum((first_page[None, :] <= local_logical[:, None]).astype(jnp.int32), axis=1) - 1
    )
    page_number = local_logical - jnp.take(first_page, page_owner)
    page_slot = jnp.take(slot_of_request, page_owner)
    page_queries = jnp.take(slot_queries, page_slot, axis=0).reshape(pool_local, head_count, HEAD)
    page_keys = pool_keys.reshape(pool_local, PAGE, head_count, HEAD)
    page_scores = (
        jnp.einsum("phd,pkhd->phk", page_queries, page_keys, preferred_element_type=jnp.float32)
        * score_scale
    )
    key_place = page_number[:, None] * PAGE + jnp.arange(PAGE, dtype=jnp.int32)[None, :]
    page_live = key_place < jnp.take(cache_length, page_owner)[:, None]
    page_scores = jnp.where(page_live[:, None, :], page_scores, NEG_FILL)
    member = page_slot[:, None] == slot_numbers[None, :]
    page_top = jnp.max(page_scores, axis=2)
    slot_top = jnp.max(jnp.where(member[:, :, None], page_top[:, None, :], NEG_FILL), axis=0)
    page_weights = jnp.exp(page_scores - jnp.take(slot_top, page_slot, axis=0)[:, :, None])
    member_weights = member.astype(jnp.float32)
    slot_total = jnp.dot(
        member_weights.T, jnp.sum(page_weights, axis=2), precision=lax.Precision.HIGHEST
    )
    page_values = pool_values.reshape(pool_local, PAGE, head_count, HEAD).astype(jnp.float32)
    page_mix = jnp.einsum(
        "phk,pkhd->phd", page_weights, page_values, precision=lax.Precision.HIGHEST
    )
    slot_mix = jnp.dot(
        member_weights.T, page_mix.reshape(pool_local, local_width), precision=lax.Precision.HIGHEST
    )
    partials = jnp.concatenate([slot_top, slot_total, slot_mix], axis=1)
    partials, prefill_received = lax.optimization_barrier((partials, prefill_received))
    received = lax.all_to_all(
        partials.reshape(dp_size, decode_rows, -1), DP, 0, 0, tiled=False
    )
    source_top = received[:, :, :head_count]
    source_total = received[:, :, head_count : 2 * head_count]
    source_mix = received[:, :, 2 * head_count :]
    mine_top = jnp.max(source_top, axis=0)
    source_factor = jnp.exp(source_top - mine_top[None])
    mine_total = jnp.sum(source_total * source_factor, axis=0)
    mine_mix = jnp.sum(
        source_mix.reshape(dp_size, decode_rows, head_count, HEAD) * source_factor[..., None], axis=0
    ).reshape(decode_rows, local_width)
    own_score = (
        jnp.einsum(
            "rhd,rhd->rh",
            own_queries.reshape(decode_rows, head_count, HEAD),
            own_keys.reshape(decode_rows, head_count, HEAD),
            preferred_element_type=jnp.float32,
        )
        * score_scale
    )
    final_top = jnp.maximum(mine_top, own_score)
    cache_factor = jnp.exp(mine_top - final_top)
    own_factor = jnp.exp(own_score - final_top)
    final_total = mine_total * cache_factor + own_factor
    final_mix = rescale(mine_mix, cache_factor, HEAD) + rescale(
        own_values.astype(jnp.float32), own_factor, HEAD
    )
    decode_attended = rescale(final_mix, 1.0 / final_total, HEAD).astype(jnp.bfloat16)
    return (
        mixed(prefill_received, prefill_tokens),
        mixed(exchange(send_shares(decode_attended)), decode_tokens),
    )


def solution(mesh):
    dp_size = mesh.shape["dp"]
    split_mesh = Mesh(
        mesh.devices.reshape(4, dp_size // 4, mesh.shape["fsdp"]), ("dy", "dz", "fsdp")
    )
    in_specs = (
        P(DP, None),
        P(DP, None),
        P(DP, "fsdp"),
        P(DP, "fsdp"),
        P(DP, "fsdp"),
        P("fsdp", DP),
        P(DP, None, "fsdp"),
        P(DP, None, "fsdp"),
        P(DP),
        P(DP, None, "fsdp"),
        P(DP, None, "fsdp"),
        P(),
        P(),
        P(),
        P(),
    )
    out_specs = (P(DP, "fsdp"), P(DP, "fsdp"))
    return jax.shard_map(
        functools.partial(per_device, dp_size=dp_size),
        mesh=split_mesh,
        in_specs=in_specs,
        out_specs=out_specs,
        check_vma=False,
    )
```

```python
import functools

import jax
import jax.numpy as jnp
from jax import lax
from jax.sharding import Mesh, PartitionSpec as P

HEAD = 128
PAGE = 128


EPSILON = 1e-05
ROPE_BASE = 10000.0
NEG_FILL = -1e30
DP = ("dy", "dz")


def layer_norm(rows_in):
    widened = rows_in.astype(jnp.float32)
    average = jnp.mean(widened, axis=-1, keepdims=True)
    centred = widened - average
    variance = jnp.mean(centred * centred, axis=-1, keepdims=True)
    return (centred * lax.rsqrt(variance + EPSILON)).astype(jnp.bfloat16)


def rotary(vectors, positions, head_size):
    row_count = vectors.shape[0]
    split_heads = vectors.reshape(row_count, -1, head_size)
    halfway = head_size // 2
    exponent = jnp.arange(halfway, dtype=jnp.float32) * (2.0 / head_size)
    frequency = jnp.power(jnp.float32(ROPE_BASE), -exponent)
    angles = positions.astype(jnp.float32)[:, None] * frequency[None, :]
    cosine = jnp.cos(angles)[:, None, :]
    sine_part = jnp.sin(angles)[:, None, :]
    leading = split_heads[..., :halfway]
    trailing = split_heads[..., halfway:]
    turned = jnp.concatenate(
        [leading * cosine - trailing * sine_part, trailing * cosine + leading * sine_part], axis=-1
    )
    return turned.reshape(row_count, -1)


def rescale(vectors, factor, head_size):
    shaped = vectors.reshape(vectors.shape[0], factor.shape[1], head_size)
    return (shaped * factor[:, :, None]).reshape(vectors.shape)


def inverse_permutation(order):
    count = order.shape[0]
    numbers = jnp.arange(count, dtype=jnp.int32)
    hit = order[None, :] == numbers[:, None]
    return jnp.sum(jnp.where(hit, numbers[None, :], 0), axis=1)


def per_device(
    prefill_tokens,
    decode_tokens,
    query_weight,
    key_weight,
    value_weight,
    out_weight,
    prior_keys,
    prior_values,
    prior_length,
    pool_keys,
    pool_values,
    page_slots,
    page_counts,
    last_fill,
    decode_request,
    *,
    dp_size,
):
    group_rows = prefill_tokens.shape[0]
    decode_rows = decode_tokens.shape[0]
    weight_rows = query_weight.shape[0]
    local_width = query_weight.shape[1]
    head_count = local_width // HEAD
    score_scale = HEAD ** (-0.5)
    data_index = lax.axis_index(DP)
    model_index = lax.axis_index("fsdp")

    decode_piece = decode_tokens.reshape(-1, local_width)
    decode_piece = jnp.pad(decode_piece, ((0, weight_rows - decode_piece.shape[0]), (0, 0)))
    bundle = jnp.stack(
        [query_weight, key_weight, value_weight, jnp.transpose(out_weight), decode_piece]
    )
    across_y = lax.all_gather(bundle, "dy", axis=1, tiled=False)
    gathered = lax.all_gather(across_y, "dz", axis=2, tiled=False).reshape(
        bundle.shape[0], dp_size * weight_rows, local_width
    )
    projection_weights = [gathered[p] for p in range(3)]
    out_columns = gathered[3]
    decode_size = decode_tokens.size
    all_decode = (
        gathered[4].reshape(dp_size, -1)[:, :decode_size].reshape(dp_size * decode_rows, -1)
    )

    def project(rows_in):
        normed = layer_norm(rows_in)
        return tuple(
            jnp.dot(normed, weight, preferred_element_type=jnp.float32)
            for weight in projection_weights
        )

    cache_length = (page_counts - 1) * PAGE + last_fill
    first_page = jnp.cumsum(page_counts) - page_counts
    request_count = decode_request.shape[0]
    slot_numbers = jnp.arange(request_count, dtype=jnp.int32)
    slot_of_request = inverse_permutation(decode_request)
    prefill_q, prefill_k, prefill_v = project(prefill_tokens)
    prefill_positions = prior_length[0] + jnp.arange(group_rows, dtype=jnp.int32)
    decode_positions = jnp.take(cache_length, decode_request)
    group_queries = rotary(prefill_q, prefill_positions, HEAD).astype(jnp.bfloat16)
    group_keys = rotary(prefill_k, prefill_positions, HEAD).astype(jnp.bfloat16)
    group_values = prefill_v.astype(jnp.bfloat16)

    prior_slots = prior_keys.shape[1]
    group_queries = group_queries.reshape(group_rows, head_count, HEAD)
    group_keys = group_keys.reshape(group_rows, head_count, HEAD)
    group_values = group_values.reshape(group_rows, head_count, HEAD)
    stored_keys = prior_keys[0].reshape(prior_slots, head_count, HEAD)
    stored_values = prior_values[0].reshape(prior_slots, head_count, HEAD)
    prior_live = jnp.arange(prior_slots, dtype=jnp.int32) < prior_length[0]

    def prefill_rows(start, count, row_queries):
        row_queries = row_queries[start : start + count]
        prior_scores = (
            jnp.einsum(
                "qhd,khd->hqk", row_queries, stored_keys, preferred_element_type=jnp.float32
            )
            * score_scale
        )
        prior_scores = jnp.where(prior_live[None, None, :], prior_scores, NEG_FILL)
        group_scores = (
            jnp.einsum(
                "qhd,khd->hqk", row_queries, group_keys, preferred_element_type=jnp.float32
            )
            * score_scale
        )
        causal = (
            jnp.arange(group_rows)[None, :] <= (start + jnp.arange(count))[:, None]
        )
        group_scores = jnp.where(causal[None], group_scores, NEG_FILL)
        row_top = jnp.maximum(
            jnp.max(prior_scores, axis=2, keepdims=True),
            jnp.max(group_scores, axis=2, keepdims=True),
        )
        prior_weights = jnp.exp(prior_scores - row_top)
        group_weights = jnp.exp(group_scores - row_top)
        weight_total = jnp.sum(prior_weights, axis=2) + jnp.sum(group_weights, axis=2)
        combined = jnp.einsum(
            "hqk,khd->qhd",
            prior_weights.astype(jnp.bfloat16),
            stored_values,
            preferred_element_type=jnp.float32,
        )
        combined = combined + jnp.einsum(
            "hqk,khd->qhd",
            group_weights.astype(jnp.bfloat16),
            group_values,
            preferred_element_type=jnp.float32,
        )
        return (
            (combined / jnp.transpose(weight_total)[:, :, None])
            .reshape(count, local_width)
            .astype(jnp.bfloat16)
        )

    model_size = out_columns.shape[0] // local_width
    column_start = model_index * local_width

    def send_shares(attended):
        terms = lax.dot_general(
            attended, out_columns, (((1,), (1,)), ((), ())), preferred_element_type=jnp.float32
        ).astype(jnp.bfloat16)
        return jnp.transpose(terms.reshape(terms.shape[0], model_size, local_width), (1, 0, 2))

    def exchange(shares):
        return lax.all_to_all(shares, "fsdp", 0, 0, tiled=False)

    def mixed(received, own_tokens):
        branch = jnp.sum(received.astype(jnp.float32), axis=0)
        residual = lax.dynamic_slice_in_dim(own_tokens, column_start, local_width, 1)
        return (residual.astype(jnp.float32) + branch).astype(jnp.bfloat16)

    half = group_rows // 2
    first_shares = send_shares(prefill_rows(0, half, group_queries))
    first_received = exchange(first_shares)
    first_shares, later_queries = lax.optimization_barrier((first_shares, group_queries))
    second_shares = send_shares(prefill_rows(half, group_rows - half, later_queries))
    second_shares, first_received, all_decode = lax.optimization_barrier(
        (second_shares, first_received, all_decode)
    )
    second_received = exchange(second_shares)
    decode_q, decode_k, decode_v = project(all_decode)
    slot_queries = rotary(decode_q, decode_positions, HEAD).astype(jnp.bfloat16)
    slot_keys = rotary(decode_k, decode_positions, HEAD).astype(jnp.bfloat16)
    slot_values = decode_v.astype(jnp.bfloat16)
    own_start = data_index * decode_rows
    own_queries = lax.dynamic_slice_in_dim(slot_queries, own_start, decode_rows, 0)
    own_keys = lax.dynamic_slice_in_dim(slot_keys, own_start, decode_rows, 0)
    own_values = lax.dynamic_slice_in_dim(slot_values, own_start, decode_rows, 0)
    pool_count = page_slots.shape[0]
    pool_local = pool_keys.shape[0]
    local_slots = data_index * pool_local + jnp.arange(pool_local, dtype=jnp.int32)
    slot_hit = page_slots[None, :] == local_slots[:, None]
    local_logical = jnp.sum(
        jnp.where(slot_hit, jnp.arange(pool_count, dtype=jnp.int32)[None, :], 0), axis=1
    )
    page_owner = (
        jnp.sum((first_page[None, :] <= local_logical[:, None]).astype(jnp.int32), axis=1) - 1
    )
    page_number = local_logical - jnp.take(first_page, page_owner)
    page_slot = jnp.take(slot_of_request, page_owner)
    page_queries = jnp.take(slot_queries, page_slot, axis=0).reshape(pool_local, head_count, HEAD)
    page_keys = pool_keys.reshape(pool_local, PAGE, head_count, HEAD)
    page_scores = (
        jnp.einsum("phd,pkhd->phk", page_queries, page_keys, preferred_element_type=jnp.float32)
        * score_scale
    )
    key_place = page_number[:, None] * PAGE + jnp.arange(PAGE, dtype=jnp.int32)[None, :]
    page_live = key_place < jnp.take(cache_length, page_owner)[:, None]
    page_scores = jnp.where(page_live[:, None, :], page_scores, NEG_FILL)
    member = page_slot[:, None] == slot_numbers[None, :]
    page_top = jnp.max(page_scores, axis=2)
    slot_top = jnp.max(jnp.where(member[:, :, None], page_top[:, None, :], NEG_FILL), axis=0)
    page_weights = jnp.exp(page_scores - jnp.take(slot_top, page_slot, axis=0)[:, :, None])
    member_weights = member.astype(jnp.float32)
    slot_total = jnp.dot(
        member_weights.T, jnp.sum(page_weights, axis=2), precision=lax.Precision.HIGHEST
    )
    page_values = pool_values.reshape(pool_local, PAGE, head_count, HEAD).astype(jnp.float32)
    page_mix = jnp.einsum(
        "phk,pkhd->phd", page_weights, page_values, precision=lax.Precision.HIGHEST
    )
    slot_mix = jnp.dot(
        member_weights.T, page_mix.reshape(pool_local, local_width), precision=lax.Precision.HIGHEST
    )
    partials = jnp.concatenate([slot_top, slot_total, slot_mix], axis=1)
    partials, second_received = lax.optimization_barrier((partials, second_received))
    received = lax.all_to_all(
        partials.reshape(dp_size, decode_rows, -1), DP, 0, 0, tiled=False
    )
    source_top = received[:, :, :head_count]
    source_total = received[:, :, head_count : 2 * head_count]
    source_mix = received[:, :, 2 * head_count :]
    mine_top = jnp.max(source_top, axis=0)
    source_factor = jnp.exp(source_top - mine_top[None])
    mine_total = jnp.sum(source_total * source_factor, axis=0)
    mine_mix = jnp.sum(
        source_mix.reshape(dp_size, decode_rows, head_count, HEAD) * source_factor[..., None], axis=0
    ).reshape(decode_rows, local_width)
    own_score = (
        jnp.einsum(
            "rhd,rhd->rh",
            own_queries.reshape(decode_rows, head_count, HEAD),
            own_keys.reshape(decode_rows, head_count, HEAD),
            preferred_element_type=jnp.float32,
        )
        * score_scale
    )
    final_top = jnp.maximum(mine_top, own_score)
    cache_factor = jnp.exp(mine_top - final_top)
    own_factor = jnp.exp(own_score - final_top)
    final_total = mine_total * cache_factor + own_factor
    final_mix = rescale(mine_mix, cache_factor, HEAD) + rescale(
        own_values.astype(jnp.float32), own_factor, HEAD
    )
    decode_attended = rescale(final_mix, 1.0 / final_total, HEAD).astype(jnp.bfloat16)
    return (
        jnp.concatenate(
            [
                mixed(first_received, prefill_tokens[:half]),
                mixed(second_received, prefill_tokens[half:]),
            ],
            axis=0,
        ),
        mixed(exchange(send_shares(decode_attended)), decode_tokens),
    )


def solution(mesh):
    dp_size = mesh.shape["dp"]
    split_mesh = Mesh(
        mesh.devices.reshape(4, dp_size // 4, mesh.shape["fsdp"]), ("dy", "dz", "fsdp")
    )
    in_specs = (
        P(DP, None),
        P(DP, None),
        P(DP, "fsdp"),
        P(DP, "fsdp"),
        P(DP, "fsdp"),
        P("fsdp", DP),
        P(DP, None, "fsdp"),
        P(DP, None, "fsdp"),
        P(DP),
        P(DP, None, "fsdp"),
        P(DP, None, "fsdp"),
        P(),
        P(),
        P(),
        P(),
    )
    out_specs = (P(DP, "fsdp"), P(DP, "fsdp"))
    return jax.shard_map(
        functools.partial(per_device, dp_size=dp_size),
        mesh=split_mesh,
        in_specs=in_specs,
        out_specs=out_specs,
        check_vma=False,
    )
```

```python
import functools

import jax
import jax.numpy as jnp
from jax import lax
from jax.sharding import Mesh, PartitionSpec as P

HEAD = 128
PAGE = 128


EPSILON = 1e-05
ROPE_BASE = 10000.0
NEG_FILL = -1e30
DP = ("dy", "dz")


def layer_norm(rows_in):
    widened = rows_in.astype(jnp.float32)
    average = jnp.mean(widened, axis=-1, keepdims=True)
    centred = widened - average
    variance = jnp.mean(centred * centred, axis=-1, keepdims=True)
    return (centred * lax.rsqrt(variance + EPSILON)).astype(jnp.bfloat16)


def rotary(vectors, positions, head_size):
    row_count = vectors.shape[0]
    split_heads = vectors.reshape(row_count, -1, head_size)
    halfway = head_size // 2
    exponent = jnp.arange(halfway, dtype=jnp.float32) * (2.0 / head_size)
    frequency = jnp.power(jnp.float32(ROPE_BASE), -exponent)
    angles = positions.astype(jnp.float32)[:, None] * frequency[None, :]
    cosine = jnp.cos(angles)[:, None, :]
    sine_part = jnp.sin(angles)[:, None, :]
    leading = split_heads[..., :halfway]
    trailing = split_heads[..., halfway:]
    turned = jnp.concatenate(
        [leading * cosine - trailing * sine_part, trailing * cosine + leading * sine_part], axis=-1
    )
    return turned.reshape(row_count, -1)


def rescale(vectors, factor, head_size):
    shaped = vectors.reshape(vectors.shape[0], factor.shape[1], head_size)
    return (shaped * factor[:, :, None]).reshape(vectors.shape)


def inverse_permutation(order):
    count = order.shape[0]
    numbers = jnp.arange(count, dtype=jnp.int32)
    hit = order[None, :] == numbers[:, None]
    return jnp.sum(jnp.where(hit, numbers[None, :], 0), axis=1)


def per_device(
    prefill_tokens,
    decode_tokens,
    query_weight,
    key_weight,
    value_weight,
    out_weight,
    prior_keys,
    prior_values,
    prior_length,
    pool_keys,
    pool_values,
    page_slots,
    page_counts,
    last_fill,
    decode_request,
    *,
    dp_size,
):
    group_rows = prefill_tokens.shape[0]
    decode_rows = decode_tokens.shape[0]
    weight_rows = query_weight.shape[0]
    local_width = query_weight.shape[1]
    head_count = local_width // HEAD
    score_scale = HEAD ** (-0.5)
    data_index = lax.axis_index(DP)
    model_index = lax.axis_index("fsdp")

    decode_piece = layer_norm(decode_tokens).reshape(-1, local_width)
    decode_piece = jnp.pad(decode_piece, ((0, weight_rows - decode_piece.shape[0]), (0, 0)))
    bundle = jnp.stack(
        [query_weight, key_weight, value_weight, jnp.transpose(out_weight), decode_piece]
    )
    across_y = lax.all_gather(bundle, "dy", axis=1, tiled=False)
    gathered = lax.all_gather(across_y, "dz", axis=2, tiled=False).reshape(
        bundle.shape[0], dp_size * weight_rows, local_width
    )
    projection_weights = [gathered[p] for p in range(3)]
    out_columns = gathered[3]
    decode_size = decode_tokens.size
    decode_normed = (
        gathered[4].reshape(dp_size, -1)[:, :decode_size].reshape(dp_size * decode_rows, -1)
    )

    def project_normed(normed):
        return tuple(
            jnp.dot(normed, weight, preferred_element_type=jnp.float32)
            for weight in projection_weights
        )

    def project(rows_in):
        return project_normed(layer_norm(rows_in))

    cache_length = (page_counts - 1) * PAGE + last_fill
    first_page = jnp.cumsum(page_counts) - page_counts
    request_count = decode_request.shape[0]
    slot_numbers = jnp.arange(request_count, dtype=jnp.int32)
    slot_of_request = inverse_permutation(decode_request)
    prefill_q, prefill_k, prefill_v = project(prefill_tokens)
    prefill_positions = prior_length[0] + jnp.arange(group_rows, dtype=jnp.int32)
    decode_positions = jnp.take(cache_length, decode_request)
    group_queries = rotary(prefill_q, prefill_positions, HEAD).astype(jnp.bfloat16)
    group_keys = rotary(prefill_k, prefill_positions, HEAD).astype(jnp.bfloat16)
    group_values = prefill_v.astype(jnp.bfloat16)

    prior_slots = prior_keys.shape[1]
    group_queries = group_queries.reshape(group_rows, head_count, HEAD)
    group_keys = group_keys.reshape(group_rows, head_count, HEAD)
    group_values = group_values.reshape(group_rows, head_count, HEAD)
    stored_keys = prior_keys[0].reshape(prior_slots, head_count, HEAD)
    stored_values = prior_values[0].reshape(prior_slots, head_count, HEAD)
    prior_scores = (
        jnp.einsum("qhd,khd->hqk", group_queries, stored_keys, preferred_element_type=jnp.float32)
        * score_scale
    )
    prior_live = jnp.arange(prior_slots, dtype=jnp.int32) < prior_length[0]
    prior_scores = jnp.where(prior_live[None, None, :], prior_scores, NEG_FILL)
    group_scores = (
        jnp.einsum("qhd,khd->hqk", group_queries, group_keys, preferred_element_type=jnp.float32)
        * score_scale
    )
    causal = jnp.arange(group_rows)[None, :] <= jnp.arange(group_rows)[:, None]
    group_scores = jnp.where(causal[None], group_scores, NEG_FILL)
    row_top = jnp.maximum(
        jnp.max(prior_scores, axis=2, keepdims=True), jnp.max(group_scores, axis=2, keepdims=True)
    )
    prior_weights = jnp.exp(prior_scores - row_top)
    group_weights = jnp.exp(group_scores - row_top)
    weight_total = jnp.sum(prior_weights, axis=2) + jnp.sum(group_weights, axis=2)
    combined = jnp.einsum(
        "hqk,khd->qhd",
        prior_weights.astype(jnp.bfloat16),
        stored_values,
        preferred_element_type=jnp.float32,
    )
    combined = combined + jnp.einsum(
        "hqk,khd->qhd",
        group_weights.astype(jnp.bfloat16),
        group_values,
        preferred_element_type=jnp.float32,
    )
    prefill_attended = (
        (combined / jnp.transpose(weight_total)[:, :, None])
        .reshape(group_rows, local_width)
        .astype(jnp.bfloat16)
    )

    model_size = out_columns.shape[0] // local_width
    column_start = model_index * local_width

    def send_shares(attended):
        terms = lax.dot_general(
            attended, out_columns, (((1,), (1,)), ((), ())), preferred_element_type=jnp.float32
        ).astype(jnp.bfloat16)
        return jnp.transpose(terms.reshape(terms.shape[0], model_size, local_width), (1, 0, 2))

    def exchange(shares):
        return lax.all_to_all(shares, "fsdp", 0, 0, tiled=False)

    def mixed(received, own_tokens):
        branch = jnp.sum(received.astype(jnp.float32), axis=0)
        residual = lax.dynamic_slice_in_dim(own_tokens, column_start, local_width, 1)
        return (residual.astype(jnp.float32) + branch).astype(jnp.bfloat16)

    prefill_shares, decode_normed = lax.optimization_barrier(
        (send_shares(prefill_attended), decode_normed)
    )
    prefill_received = exchange(prefill_shares)
    decode_q, decode_k, decode_v = project_normed(decode_normed)
    slot_queries = rotary(decode_q, decode_positions, HEAD).astype(jnp.bfloat16)
    slot_keys = rotary(decode_k, decode_positions, HEAD).astype(jnp.bfloat16)
    slot_values = decode_v.astype(jnp.bfloat16)
    own_start = data_index * decode_rows
    own_queries = lax.dynamic_slice_in_dim(slot_queries, own_start, decode_rows, 0)
    own_keys = lax.dynamic_slice_in_dim(slot_keys, own_start, decode_rows, 0)
    own_values = lax.dynamic_slice_in_dim(slot_values, own_start, decode_rows, 0)
    pool_count = page_slots.shape[0]
    pool_local = pool_keys.shape[0]
    local_slots = data_index * pool_local + jnp.arange(pool_local, dtype=jnp.int32)
    slot_hit = page_slots[None, :] == local_slots[:, None]
    local_logical = jnp.sum(
        jnp.where(slot_hit, jnp.arange(pool_count, dtype=jnp.int32)[None, :], 0), axis=1
    )
    page_owner = (
        jnp.sum((first_page[None, :] <= local_logical[:, None]).astype(jnp.int32), axis=1) - 1
    )
    page_number = local_logical - jnp.take(first_page, page_owner)
    page_slot = jnp.take(slot_of_request, page_owner)
    page_queries = jnp.take(slot_queries, page_slot, axis=0).reshape(pool_local, head_count, HEAD)
    page_keys = pool_keys.reshape(pool_local, PAGE, head_count, HEAD)
    page_scores = (
        jnp.einsum("phd,pkhd->phk", page_queries, page_keys, preferred_element_type=jnp.float32)
        * score_scale
    )
    key_place = page_number[:, None] * PAGE + jnp.arange(PAGE, dtype=jnp.int32)[None, :]
    page_live = key_place < jnp.take(cache_length, page_owner)[:, None]
    page_scores = jnp.where(page_live[:, None, :], page_scores, NEG_FILL)
    member = page_slot[:, None] == slot_numbers[None, :]
    page_top = jnp.max(page_scores, axis=2)
    slot_top = jnp.max(jnp.where(member[:, :, None], page_top[:, None, :], NEG_FILL), axis=0)
    page_weights = jnp.exp(page_scores - jnp.take(slot_top, page_slot, axis=0)[:, :, None])
    member_weights = member.astype(jnp.float32)
    slot_total = jnp.dot(
        member_weights.T, jnp.sum(page_weights, axis=2), precision=lax.Precision.HIGHEST
    )
    page_values = pool_values.reshape(pool_local, PAGE, head_count, HEAD).astype(jnp.float32)
    page_mix = jnp.einsum(
        "phk,pkhd->phd", page_weights, page_values, precision=lax.Precision.HIGHEST
    )
    slot_mix = jnp.dot(
        member_weights.T, page_mix.reshape(pool_local, local_width), precision=lax.Precision.HIGHEST
    )
    partials = jnp.concatenate([slot_top, slot_total, slot_mix], axis=1)
    partials, prefill_received = lax.optimization_barrier((partials, prefill_received))
    received = lax.all_to_all(
        partials.reshape(dp_size, decode_rows, -1), DP, 0, 0, tiled=False
    )
    source_top = received[:, :, :head_count]
    source_total = received[:, :, head_count : 2 * head_count]
    source_mix = received[:, :, 2 * head_count :]
    mine_top = jnp.max(source_top, axis=0)
    source_factor = jnp.exp(source_top - mine_top[None])
    mine_total = jnp.sum(source_total * source_factor, axis=0)
    mine_mix = jnp.sum(
        source_mix.reshape(dp_size, decode_rows, head_count, HEAD) * source_factor[..., None], axis=0
    ).reshape(decode_rows, local_width)
    own_score = (
        jnp.einsum(
            "rhd,rhd->rh",
            own_queries.reshape(decode_rows, head_count, HEAD),
            own_keys.reshape(decode_rows, head_count, HEAD),
            preferred_element_type=jnp.float32,
        )
        * score_scale
    )
    final_top = jnp.maximum(mine_top, own_score)
    cache_factor = jnp.exp(mine_top - final_top)
    own_factor = jnp.exp(own_score - final_top)
    final_total = mine_total * cache_factor + own_factor
    final_mix = rescale(mine_mix, cache_factor, HEAD) + rescale(
        own_values.astype(jnp.float32), own_factor, HEAD
    )
    decode_attended = rescale(final_mix, 1.0 / final_total, HEAD).astype(jnp.bfloat16)
    return (
        mixed(prefill_received, prefill_tokens),
        mixed(exchange(send_shares(decode_attended)), decode_tokens),
    )


def solution(mesh):
    dp_size = mesh.shape["dp"]
    split_mesh = Mesh(
        mesh.devices.reshape(4, dp_size // 4, mesh.shape["fsdp"]), ("dy", "dz", "fsdp")
    )
    in_specs = (
        P(DP, None),
        P(DP, None),
        P(DP, "fsdp"),
        P(DP, "fsdp"),
        P(DP, "fsdp"),
        P("fsdp", DP),
        P(DP, None, "fsdp"),
        P(DP, None, "fsdp"),
        P(DP),
        P(DP, None, "fsdp"),
        P(DP, None, "fsdp"),
        P(),
        P(),
        P(),
        P(),
    )
    out_specs = (P(DP, "fsdp"), P(DP, "fsdp"))
    return jax.shard_map(
        functools.partial(per_device, dp_size=dp_size),
        mesh=split_mesh,
        in_specs=in_specs,
        out_specs=out_specs,
        check_vma=False,
    )
```
